256 devices in a mesh: sub: 16 (over y, z_lo), grp: 16 (over x, z_hi, core).
Axes of the slice: x: 4, y: 4, z: 8 (z_hi: 2, z_lo: 4; z = z_hi * 4 + z_lo), core: 2. Of those that a mesh axis runs over, the one named last changes fastest.
Arguments:
- facies: int32 [256, 128, 128], P('sub', 'grp'), may hold values from 0 to 7
- facies_perm: float32 [8], replicated, may hold values from 0.2 to 5
- perm_scale: float32 [256, 128, 128], P('sub', 'grp'), may hold values from 0.5 to 2
- source: float32 [256, 128, 128], P('sub', 'grp'), may hold values from -6 to 6
- pressure_start: float32 [256, 128, 128], P('sub', 'grp'), may hold values from -4 to 4
- intersection_depth: int32 [15], replicated, may hold values from 1 to 4, as said below
Outputs:
- pressure: float32 [256, 128, 128], P('sub', 'grp')
The draws below stay inside these ranges and needn't reach their ends.
Inputs may be any that keep to these rules, and one draw needn't show every extreme that they name: `intersection_depth`: every entry is a margin depth; some entry equals 4 in every draw.
All inputs are finite; a program needn't handle non-finite values.
Results may differ from the reference program's by a relative error of at most 0.0003.
Values sent between devices are 32-bit elements; how exact they have to be, the bound alone decides.
No kernel may reach another device: no remote copies, remote signals or barrier semaphores. Data moves between devices by JAX's collectives and lax.ppermute only.
A program may use at most 64 MiB of HBM per device.

```python
import math
import jax
import jax.numpy as jnp
from jax import lax

CZ = 16
NY = 128
OV = 4
BL = 8
ROUNDS = 4
OUTER = 2
FACIES = 8
NZ = 256
NX = 128
PAIRS = 15
N_SUB = 16


def draw_intersection_depth(key, part):
    depths = jax.random.randint(key, (PAIRS,), 1, OV + 1)
    chosen = jax.random.randint(jax.random.fold_in(key, 7), (), 0, PAIRS)
    return jnp.where(jnp.arange(PAIRS) == chosen, OV, depths).astype(jnp.int32)


def touch_ends(array, rng, low, largest):
    index_at = [jax.random.randint(jax.random.fold_in(rng, axis), (), 0, length) for axis, length in enumerate(array.shape)]
    main_axis = array.shape.index(max(array.shape))
    beside = index_at[:main_axis] + [(index_at[main_axis] + 1) % array.shape[main_axis]] + index_at[main_axis + 1:]
    return array.at[tuple(index_at)].set(low).at[tuple(beside)].set(largest)


def level_of(own_key, shape, pieces, low, top_value):
    loudness, own = 1.0, jax.random.fold_in(own_key, 6)
    for dim, shards_of in pieces:
        steps = jnp.exp(jax.random.uniform(jax.random.fold_in(own, dim), (shards_of,), jnp.float32, low / len(pieces), top_value / len(pieces)))
        loudness = loudness * jnp.repeat(steps, shape[dim] // shards_of).reshape([-1 if axis == dim else 1 for axis in range(len(shape))])
    return loudness


def normal_values(key, dims, spread, limit, shards=(), kind=jnp.bfloat16):
    factor_of = level_of(key, dims, shards, -0.22, 0.18) if shards else 1.0
    values = jax.random.normal(key, dims, jnp.float32) * spread * factor_of
    return jnp.minimum(jnp.maximum(values, -limit), limit).astype(kind)


def setup_inputs(seed: int = 0) -> dict:
    key_list = jax.random.split(jax.random.key(seed), 7)
    return {
        "facies": touch_ends(jax.random.randint(key_list[0], (NZ, NX, NY), 0, FACIES), jax.random.fold_in(key_list[0], 1), 0, FACIES - 1).astype(jnp.int32),
        "facies_perm": jnp.clip(jnp.exp(jax.random.uniform(key_list[1], (FACIES,), jnp.float32, math.log(0.2), math.log(5.0))), 0.2, 5.0),
        "perm_scale": jnp.clip(jnp.exp(math.log(2.0) - 1.3862944 * jax.random.uniform(key_list[2], (NZ, NX, NY), jnp.float32) ** level_of(key_list[2], (NZ, NX, NY), ((0, 16), (1, 16)), -0.2, 0.2)), 0.5, 2.0),
        "source": normal_values(key_list[3], (NZ, NX, NY), 1.0, 6.0, ((0, 16), (1, 16)), jnp.float32),
        "pressure_start": normal_values(key_list[4], (NZ, NX, NY), 0.5, 4.0, ((0, 16), (1, 16)), jnp.float32),
        "intersection_depth": draw_intersection_depth(jax.random.fold_in(key_list[6], 71), 0),
    }


STORE = 0.02


def relax_weight(round_index):
    return 1.0 / (1.4 + 0.6 * math.cos(math.pi * (2 * round_index + 1) / (2 * ROUNDS)))


def harmonic(former, second):
    inside = jnp.where((former > 0) & (second > 0), 1.0, 0.0)
    safe_former = jnp.where(former > 0, former, 1.0)
    safe_second = jnp.where(second > 0, second, 1.0)
    return inside * (2.0 * safe_former * safe_second / (safe_former + safe_second))


def neighbours(field, line_axis):
    extent = field.shape[line_axis]
    zero_plane = jnp.zeros_like(lax.slice_in_dim(field, 0, 1, axis=line_axis))
    lower_side = jnp.concatenate([zero_plane, lax.slice_in_dim(field, 0, extent - 1, axis=line_axis)], axis=line_axis)
    upper_side = jnp.concatenate([lax.slice_in_dim(field, 1, extent, axis=line_axis), zero_plane], axis=line_axis)
    return lower_side, upper_side


def apply_operator(coeffs, center, below_rows, above_rows, left_side, right_side):
    diagonal, face_below, face_above, face_left, face_right, face_front, face_back = coeffs
    front_cols, back_cols = neighbours(center, 2)
    coupled = face_below * below_rows + face_above * above_rows + face_left * left_side + face_right * right_side + face_front * front_cols + face_back * back_cols
    return diagonal * center - coupled


def operate(coeffs, field):
    below_rows, above_rows = neighbours(field, 0)
    left_side, right_side = neighbours(field, 1)
    return apply_operator(coeffs, field, below_rows, above_rows, left_side, right_side)


def pack_lines(field, line_axis):
    extents = field.shape
    split_dims = extents[:line_axis] + (extents[line_axis] // BL, BL) + extents[line_axis + 1:]
    return jnp.moveaxis(field.reshape(split_dims), line_axis + 1, 0).reshape(BL, -1)


def unpack_lines(packed, line_axis, extents):
    split_dims = extents[:line_axis] + (extents[line_axis] // BL, BL) + extents[line_axis + 1:]
    moved_dims = (BL,) + split_dims[:line_axis + 1] + split_dims[line_axis + 2:]
    return jnp.moveaxis(packed.reshape(moved_dims), 0, line_axis + 1).reshape(extents)


def factor_lines(lower_band, middle, upper_band):
    pivots = [middle[0]]
    multipliers = [jnp.zeros_like(middle[0])]
    for position in range(1, BL):
        multiplier = lower_band[position] / pivots[position - 1]
        multipliers.append(multiplier)
        pivots.append(middle[position] - multiplier * upper_band[position - 1])
    return jnp.stack(multipliers), 1.0 / jnp.stack(pivots), upper_band


def solve_lines(factors, packed_rhs):
    multipliers, inverse, upper_band = factors
    forward = [packed_rhs[0]]
    for position in range(1, BL):
        forward.append(packed_rhs[position] - multipliers[position] * forward[position - 1])
    result = [None] * BL
    result[BL - 1] = forward[BL - 1] * inverse[BL - 1]
    for position in range(BL - 2, -1, -1):
        result[position] = (forward[position] - upper_band[position] * result[position + 1]) * inverse[position]
    return jnp.stack(result)


def line_factors(coeffs, active, line_axis):
    diagonal = coeffs[0]
    face_low = coeffs[2 * line_axis + 1]
    face_high = coeffs[2 * line_axis + 2]
    extent = diagonal.shape[line_axis]
    broadcast_shape = [1, 1, 1]
    broadcast_shape[line_axis] = extent
    position = (jnp.arange(extent, dtype=jnp.int32) % BL).reshape(broadcast_shape)
    if line_axis == 0:
        active_low, active_high = neighbours(active, 0)
    else:
        active_low = active
        active_high = active
    lower_band = jnp.where(position != 0, -face_low * active * active_low, 0.0)
    upper_band = jnp.where(position != BL - 1, -face_high * active * active_high, 0.0)
    middle = jnp.where(active > 0, diagonal, 1.0)
    return factor_lines(pack_lines(lower_band, line_axis), pack_lines(middle, line_axis), pack_lines(upper_band, line_axis))


def correction_step(factors, line_axis, update, weight_now, estimate):
    solved = solve_lines(factors, pack_lines(update, line_axis))
    return estimate + weight_now * unpack_lines(solved, line_axis, estimate.shape)


def reference(facies, facies_perm, perm_scale, source, pressure_start, intersection_depth):
    permeability = facies_perm[facies] * perm_scale
    padded = jnp.pad(permeability, 1)
    faces_vertical = harmonic(padded[:-1, 1:-1, 1:-1], padded[1:, 1:-1, 1:-1])
    faces_across = harmonic(padded[1:-1, :-1, 1:-1], padded[1:-1, 1:, 1:-1])
    faces_along = harmonic(padded[1:-1, 1:-1, :-1], padded[1:-1, 1:-1, 1:])
    face_below = faces_vertical[:-1]
    face_above = faces_vertical[1:]
    face_left = faces_across[:, :-1]
    face_right = faces_across[:, 1:]
    face_front = faces_along[:, :, :-1]
    face_back = faces_along[:, :, 1:]
    diagonal = STORE + face_below + face_above + face_left + face_right + face_front + face_back
    coeffs = (diagonal, face_below, face_above, face_left, face_right, face_front, face_back)
    margin_rows = CZ + 2 * OV
    padded_coeffs = tuple(jnp.pad(member, ((OV, OV), (0, 0), (0, 0))) for member in coeffs)
    bounds = jnp.concatenate([jnp.zeros((1,), jnp.int32), intersection_depth.astype(jnp.int32), jnp.zeros((1,), jnp.int32)])
    offsets = jnp.arange(margin_rows, dtype=jnp.int32) - OV
    pressure = pressure_start
    for outer_turn in range(OUTER):
        residual = source - operate(coeffs, pressure)
        residual_pad = jnp.pad(residual, ((OV, OV), (0, 0), (0, 0)))

        def one_slab(slab_index, combined):
            start = (slab_index * CZ).astype(jnp.int32)
            local = tuple(lax.dynamic_slice_in_dim(member, start, margin_rows, 0) for member in padded_coeffs)
            target = lax.dynamic_slice_in_dim(residual_pad, start, margin_rows, 0)
            depth_low = bounds[slab_index]
            depth_high = bounds[slab_index + 1]
            inside_slab = (offsets >= -depth_low) & (offsets < CZ + depth_high)
            band_rows = (offsets < depth_low) | (offsets >= CZ - depth_high)
            active = jnp.where(inside_slab, 1.0, 0.0).reshape(margin_rows, 1, 1)
            weight = jnp.where(inside_slab & band_rows, 0.5, jnp.where(inside_slab, 1.0, 0.0)).reshape(margin_rows, 1, 1)
            target = target * active
            factors_x = line_factors(local, active, 1)
            factors_y = line_factors(local, active, 2)
            factors_z = line_factors(local, active, 0)
            estimate = jnp.zeros_like(target)
            for round_index in range(ROUNDS):
                weight_now = relax_weight(round_index)
                for factors, line_axis in ((factors_x, 1), (factors_y, 2), (factors_z, 0)):
                    update = active * (target - operate(local, estimate))
                    estimate = correction_step(factors, line_axis, update, weight_now, estimate)
            piece = lax.dynamic_slice_in_dim(combined, start, margin_rows, 0) + weight * estimate
            return lax.dynamic_update_slice_in_dim(combined, piece, start, 0)

        combined = lax.fori_loop(0, N_SUB, one_slab, jnp.zeros((NZ + 2 * OV, NX, NY), jnp.float32))
        pressure = pressure + combined[OV:OV + NZ]
    return pressure
```

```python
import math

import jax
import jax.numpy as jnp
from jax import lax
from jax.sharding import PartitionSpec as P

OV = 4
BL = 8
ROUNDS = 4
OUTER = 2
FACIES = 8


STORE = 0.02


def relax_weight(round_index):
    return 1.0 / (1.4 + 0.6 * math.cos(math.pi * (2 * round_index + 1) / (2 * ROUNDS)))


def harmonic(former, second):
    inside = jnp.where((former > 0) & (second > 0), 1.0, 0.0)
    safe_former = jnp.where(former > 0, former, 1.0)
    safe_second = jnp.where(second > 0, second, 1.0)
    return inside * (2.0 * safe_former * safe_second / (safe_former + safe_second))


def lower_nb(field, axis, fill=0.0):
    extent = field.shape[axis]
    plane = jnp.full_like(lax.slice_in_dim(field, 0, 1, axis=axis), fill)
    return jnp.concatenate([plane, lax.slice_in_dim(field, 0, extent - 1, axis=axis)], axis=axis)


def upper_nb(field, axis, fill=0.0):
    extent = field.shape[axis]
    plane = jnp.full_like(lax.slice_in_dim(field, 0, 1, axis=axis), fill)
    return jnp.concatenate([lax.slice_in_dim(field, 1, extent, axis=axis), plane], axis=axis)


def apply_operator(coeffs, center):
    diagonal, face_below, face_above, face_left, face_right, face_front, face_back = coeffs
    coupled = (
        face_below * lower_nb(center, 0)
        + face_above * upper_nb(center, 0)
        + face_left * lower_nb(center, 1)
        + face_right * upper_nb(center, 1)
        + face_front * lower_nb(center, 2)
        + face_back * upper_nb(center, 2)
    )
    return diagonal * center - coupled


def block_position(shape, axis):
    broadcast_shape = [1] * len(shape)
    broadcast_shape[axis] = shape[axis]
    return (jnp.arange(shape[axis], dtype=jnp.int32) % BL).reshape(broadcast_shape)


def factor_lines(lower_band, middle, upper_band, axis):
    upper_prev = lower_nb(upper_band, axis)
    pivots = middle
    for _ in range(BL - 1):
        pivots = middle - (lower_band / lower_nb(pivots, axis, 1.0)) * upper_prev
    multipliers = lower_band / lower_nb(pivots, axis, 1.0)
    return (multipliers, 1.0 / pivots, upper_band, axis)


def solve_lines(factors, rhs):
    multipliers, inverse, upper_band, axis = factors
    forward = rhs
    for _ in range(BL - 1):
        forward = rhs - multipliers * lower_nb(forward, axis)
    result = forward * inverse
    for _ in range(BL - 1):
        result = (forward - upper_band * upper_nb(result, axis)) * inverse
    return result


def line_factors(coeffs, active, axis):
    diagonal = coeffs[0]
    line_axis = {0: 0, 1: 1, 2: 2}[axis]
    face_low = coeffs[2 * line_axis + 1]
    face_high = coeffs[2 * line_axis + 2]
    position = block_position(diagonal.shape, axis)
    if axis == 0:
        active_low = lower_nb(active, 0)
        active_high = upper_nb(active, 0)
    else:
        active_low = active
        active_high = active
    lower_band = jnp.where(position != 0, -face_low * active * active_low, 0.0)
    upper_band = jnp.where(position != BL - 1, -face_high * active * active_high, 0.0)
    middle = jnp.where(active > 0, diagonal, 1.0)
    return factor_lines(lower_band, middle, upper_band, axis)


def grp_pairs(axis, by):
    devices = lax.axis_size(axis)
    return [(i, i + by) for i in range(devices) if 0 <= i + by < devices]


def with_sides(value, axis, dim):
    from_left = lax.ppermute(value, axis, grp_pairs(axis, 1))
    from_right = lax.ppermute(value, axis, grp_pairs(axis, -1))
    return jnp.concatenate([from_left, value, from_right], axis=dim)


def with_rows(value, axis, dim, width):
    length = value.shape[dim]
    below = lax.ppermute(
        lax.slice_in_dim(value, length - width, length, axis=dim), axis, grp_pairs(axis, 1)
    )
    above = lax.ppermute(lax.slice_in_dim(value, 0, width, axis=dim), axis, grp_pairs(axis, -1))
    return jnp.concatenate([below, value, above], axis=dim)


def on_device(facies, facies_perm, perm_scale, source, pressure_start, intersection_depth):
    slab_rows, tile_cols, line_cells = source.shape
    margin_rows = slab_rows + 2 * OV
    perm_local = jnp.zeros(source.shape, jnp.float32)
    for facies_kind in range(FACIES):
        perm_local = perm_local + jnp.where(facies == facies_kind, facies_perm[facies_kind], 0.0)
    perm_local = perm_local * perm_scale

    stacked = jnp.stack([perm_local, pressure_start, source])
    stacked = with_rows(stacked, "sub", 1, OV + 1)
    stacked = with_sides(stacked, "grp", 2)
    perm_wide = stacked[0]
    pressure_wide = stacked[1]
    source_wide = stacked[2][1:-1]

    faces_vertical = harmonic(perm_wide[:-1], perm_wide[1:])
    middle_block = perm_wide[1:-1]
    faces_across = harmonic(middle_block[:, :-1], middle_block[:, 1:])
    faces_along = harmonic(middle_block[:, :, :-1], middle_block[:, :, 1:])
    zero_col = jnp.zeros_like(middle_block[:, :1])
    zero_lane = jnp.zeros_like(middle_block[:, :, :1])
    face_below = faces_vertical[:-1]
    face_above = faces_vertical[1:]
    face_left = jnp.concatenate([zero_col, faces_across], axis=1)
    face_right = jnp.concatenate([faces_across, zero_col], axis=1)
    face_front = jnp.concatenate([zero_lane, faces_along], axis=2)
    face_back = jnp.concatenate([faces_along, zero_lane], axis=2)
    diagonal = STORE + face_below + face_above + face_left + face_right + face_front + face_back
    coeffs = (diagonal, face_below, face_above, face_left, face_right, face_front, face_back)
    own = slice(tile_cols, 2 * tile_cols)
    own_coeffs = tuple(member[:, own] for member in coeffs)

    slab_index = lax.axis_index("sub")
    bounds = jnp.concatenate(
        [jnp.zeros((1,), jnp.int32), intersection_depth, jnp.zeros((1,), jnp.int32)]
    )
    depth_low = bounds[slab_index]
    depth_high = bounds[slab_index + 1]
    offsets = jnp.arange(margin_rows, dtype=jnp.int32) - OV
    inside_slab = (offsets >= -depth_low) & (offsets < slab_rows + depth_high)
    band_rows = (offsets < depth_low) | (offsets >= slab_rows - depth_high)
    active = jnp.where(inside_slab, 1.0, 0.0).reshape(margin_rows, 1, 1)
    weight = jnp.where(inside_slab & band_rows, 0.5, jnp.where(inside_slab, 1.0, 0.0)).reshape(
        margin_rows, 1, 1
    )
    full_active = jnp.broadcast_to(active, diagonal.shape)
    own_active = jnp.broadcast_to(active, own_coeffs[0].shape)
    factors_x = line_factors(own_coeffs, own_active, 1)
    factors_y = line_factors(coeffs, full_active, 2)
    factors_z = line_factors(coeffs, full_active, 0)

    rows_pad = jnp.zeros_like(pressure_wide[:1])
    for outer_turn in range(OUTER):
        center = pressure_wide[1:-1]
        coupled = (
            face_below * pressure_wide[:-2]
            + face_above * pressure_wide[2:]
            + face_left * lower_nb(center, 1)
            + face_right * upper_nb(center, 1)
            + face_front * lower_nb(center, 2)
            + face_back * upper_nb(center, 2)
        )
        residual = source_wide - (diagonal * center - coupled)
        target = residual * active
        estimate = None
        for round_index in range(ROUNDS):
            weight_now = relax_weight(round_index)
            if estimate is None:
                update_own = target[:, own]
                estimate_own = weight_now * solve_lines(factors_x, update_own)
            else:
                update = active * (target - apply_operator(coeffs, estimate))
                estimate_own = estimate[:, own] + weight_now * solve_lines(
                    factors_x, update[:, own]
                )
            estimate = with_sides(estimate_own, "grp", 1)
            for factors in (factors_y, factors_z):
                update = active * (target - apply_operator(coeffs, estimate))
                estimate = estimate + weight_now * solve_lines(factors, update)
        correction = weight * estimate
        if outer_turn + 1 < OUTER:
            span = 2 * OV + 1
            from_below = lax.ppermute(
                correction[margin_rows - span :], "sub", grp_pairs("sub", 1)
            )
            from_above = lax.ppermute(correction[:span], "sub", grp_pairs("sub", -1))
            filler = jnp.zeros(
                (margin_rows + 2 - span,) + correction.shape[1:], jnp.float32
            )
            pressure_wide = (
                pressure_wide
                + jnp.concatenate([rows_pad, correction, rows_pad], axis=0)
                + jnp.concatenate([from_below, filler], axis=0)
                + jnp.concatenate([filler, from_above], axis=0)
            )
        else:
            own_corr = correction[:, own]
            from_below = lax.ppermute(
                own_corr[margin_rows - OV :], "sub", grp_pairs("sub", 1)
            )
            from_above = lax.ppermute(own_corr[:OV], "sub", grp_pairs("sub", -1))
            filler = jnp.zeros((slab_rows - OV, tile_cols, line_cells), jnp.float32)
            combined = (
                own_corr[OV : OV + slab_rows]
                + jnp.concatenate([from_below, filler], axis=0)
                + jnp.concatenate([filler, from_above], axis=0)
            )
            return pressure_wide[OV + 1 : OV + 1 + slab_rows, own] + combined


def solution(mesh):
    return jax.shard_map(
        on_device,
        mesh=mesh,
        in_specs=(
            P("sub", "grp", None),
            P(),
            P("sub", "grp", None),
            P("sub", "grp", None),
            P("sub", "grp", None),
            P(),
        ),
        out_specs=P("sub", "grp", None),
        check_vma=False,
    )
```

```python
import math

import jax
import jax.numpy as jnp
from jax import lax
from jax.sharding import PartitionSpec as P
from jax.experimental import pallas as pl
from jax.experimental.pallas import tpu as pltpu

OV = 4
BL = 8
ROUNDS = 4
OUTER = 2
FACIES = 8


STORE = 0.02


def relax_weight(round_index):
    return 1.0 / (1.4 + 0.6 * math.cos(math.pi * (2 * round_index + 1) / (2 * ROUNDS)))


def harmonic(former, second):
    inside = jnp.where((former > 0) & (second > 0), 1.0, 0.0)
    safe_former = jnp.where(former > 0, former, 1.0)
    safe_second = jnp.where(second > 0, second, 1.0)
    return inside * (2.0 * safe_former * safe_second / (safe_former + safe_second))


def lower_nb(field, axis, fill=0.0):
    extent = field.shape[axis]
    plane = jnp.full_like(lax.slice_in_dim(field, 0, 1, axis=axis), fill)
    return jnp.concatenate([plane, lax.slice_in_dim(field, 0, extent - 1, axis=axis)], axis=axis)


def upper_nb(field, axis, fill=0.0):
    extent = field.shape[axis]
    plane = jnp.full_like(lax.slice_in_dim(field, 0, 1, axis=axis), fill)
    return jnp.concatenate([lax.slice_in_dim(field, 1, extent, axis=axis), plane], axis=axis)


def apply_operator(coeffs, center):
    diagonal, face_below, face_above, face_left, face_right, face_front, face_back = coeffs
    coupled = (
        face_below * lower_nb(center, 0)
        + face_above * upper_nb(center, 0)
        + face_left * lower_nb(center, 1)
        + face_right * upper_nb(center, 1)
        + face_front * lower_nb(center, 2)
        + face_back * upper_nb(center, 2)
    )
    return diagonal * center - coupled


def block_position(shape, axis):
    broadcast_shape = [1] * len(shape)
    broadcast_shape[axis] = shape[axis]
    return (jnp.arange(shape[axis], dtype=jnp.int32) % BL).reshape(broadcast_shape)


def factor_lines(lower_band, middle, upper_band, axis):
    upper_prev = lower_nb(upper_band, axis)
    pivots = middle
    for _ in range(BL - 1):
        pivots = middle - (lower_band / lower_nb(pivots, axis, 1.0)) * upper_prev
    multipliers = lower_band / lower_nb(pivots, axis, 1.0)
    return (multipliers, 1.0 / pivots, upper_band, axis)


def solve_lines(factors, rhs):
    multipliers, inverse, upper_band, axis = factors
    forward = rhs
    for _ in range(BL - 1):
        forward = rhs - multipliers * lower_nb(forward, axis)
    result = forward * inverse
    for _ in range(BL - 1):
        result = (forward - upper_band * upper_nb(result, axis)) * inverse
    return result


def line_factors(coeffs, active, axis):
    diagonal = coeffs[0]
    line_axis = {0: 0, 1: 1, 2: 2}[axis]
    face_low = coeffs[2 * line_axis + 1]
    face_high = coeffs[2 * line_axis + 2]
    position = block_position(diagonal.shape, axis)
    if axis == 0:
        active_low = lower_nb(active, 0)
        active_high = upper_nb(active, 0)
    else:
        active_low = active
        active_high = active
    lower_band = jnp.where(position != 0, -face_low * active * active_low, 0.0)
    upper_band = jnp.where(position != BL - 1, -face_high * active * active_high, 0.0)
    middle = jnp.where(active > 0, diagonal, 1.0)
    return factor_lines(lower_band, middle, upper_band, axis)


def make_round_kernel(weight_now, weight_next, last, own_cols):
    def kernel(
        e_ref, t_ref, d_ref, fb_ref, fa_ref, fl_ref, fr_ref, ff_ref, fk_ref, act_ref,
        ym_ref, yi_ref, yu_ref, zm_ref, zi_ref, zu_ref, xm_ref, xi_ref, xu_ref,
        o_ref, s_ref, f_ref,
    ):
        rows, cols, lanes = e_ref.shape

        def row_lower(x):
            return jnp.concatenate([jnp.zeros_like(x[:1]), x[:-1]], axis=0)

        def row_upper(x):
            return jnp.concatenate([x[1:], jnp.zeros_like(x[:1])], axis=0)

        def operate(e):
            coupled = (
                fb_ref[...] * row_lower(e)
                + fa_ref[...] * row_upper(e)
                + fl_ref[...] * pltpu.roll(e, 1, 1)
                + fr_ref[...] * pltpu.roll(e, cols - 1, 1)
                + ff_ref[...] * pltpu.roll(e, 1, 2)
                + fk_ref[...] * pltpu.roll(e, lanes - 1, 2)
            )
            return d_ref[...] * e - coupled

        def roll_solve(rhs, m, inv, u, axis, extent):
            forward = rhs
            for _ in range(BL - 1):
                forward = rhs - m * pltpu.roll(forward, 1, axis)
            result = forward * inv
            for _ in range(BL - 1):
                result = (forward - u * pltpu.roll(result, extent - 1, axis)) * inv
            return result

        act = act_ref[...]
        target = t_ref[...]
        e = e_ref[...]
        update = act * (target - operate(e))
        e = e + weight_now * roll_solve(update, ym_ref[...], yi_ref[...], yu_ref[...], 2, lanes)
        s_ref[...] = act * (target - operate(e))
        for block in range(rows // BL):
            base = block * BL
            forward = s_ref[base]
            f_ref[base] = forward
            for position in range(1, BL):
                r = base + position
                forward = s_ref[r] - zm_ref[r] * forward
                f_ref[r] = forward
            result = forward * zi_ref[base + BL - 1]
            s_ref[base + BL - 1] = result
            for position in range(BL - 2, -1, -1):
                r = base + position
                result = (f_ref[r] - zu_ref[r] * result) * zi_ref[r]
                s_ref[r] = result
        e = e + weight_now * s_ref[...]
        if last:
            o_ref[...] = e
        else:
            update = (act * (target - operate(e)))[:, own_cols]
            o_ref[...] = e[:, own_cols] + weight_next * roll_solve(
                update, xm_ref[...], xi_ref[...], xu_ref[...], 1, BL
            )

    return kernel


def round_call(weight_now, weight_next, last, tile_cols, estimate, target, coeffs, active, fy, fz, fx):
    own_cols = slice(tile_cols, 2 * tile_cols)
    shape = estimate.shape
    out_shape = shape if last else (shape[0], tile_cols, shape[2])
    return pl.pallas_call(
        make_round_kernel(weight_now, weight_next, last, own_cols),
        out_shape=jax.ShapeDtypeStruct(out_shape, jnp.float32),
        scratch_shapes=[pltpu.VMEM(shape, jnp.float32), pltpu.VMEM(shape, jnp.float32)],
    )(estimate, target, *coeffs, active, *fy[:3], *fz[:3], *fx[:3])


def grp_pairs(axis, by):
    devices = lax.axis_size(axis)
    return [(i, i + by) for i in range(devices) if 0 <= i + by < devices]


def with_sides(value, axis, dim):
    from_left = lax.ppermute(value, axis, grp_pairs(axis, 1))
    from_right = lax.ppermute(value, axis, grp_pairs(axis, -1))
    return jnp.concatenate([from_left, value, from_right], axis=dim)


def with_rows(value, axis, dim, width):
    length = value.shape[dim]
    below = lax.ppermute(
        lax.slice_in_dim(value, length - width, length, axis=dim), axis, grp_pairs(axis, 1)
    )
    above = lax.ppermute(lax.slice_in_dim(value, 0, width, axis=dim), axis, grp_pairs(axis, -1))
    return jnp.concatenate([below, value, above], axis=dim)


def on_device(facies, facies_perm, perm_scale, source, pressure_start, intersection_depth):
    slab_rows, tile_cols, line_cells = source.shape
    margin_rows = slab_rows + 2 * OV
    perm_local = jnp.zeros(source.shape, jnp.float32)
    for facies_kind in range(FACIES):
        perm_local = perm_local + jnp.where(facies == facies_kind, facies_perm[facies_kind], 0.0)
    perm_local = perm_local * perm_scale

    stacked = jnp.stack([perm_local, pressure_start, source])
    stacked = with_rows(stacked, "sub", 1, OV + 1)
    stacked = with_sides(stacked, "grp", 2)
    perm_wide = stacked[0]
    pressure_wide = stacked[1]
    source_wide = stacked[2][1:-1]

    faces_vertical = harmonic(perm_wide[:-1], perm_wide[1:])
    middle_block = perm_wide[1:-1]
    faces_across = harmonic(middle_block[:, :-1], middle_block[:, 1:])
    faces_along = harmonic(middle_block[:, :, :-1], middle_block[:, :, 1:])
    zero_col = jnp.zeros_like(middle_block[:, :1])
    zero_lane = jnp.zeros_like(middle_block[:, :, :1])
    face_below = faces_vertical[:-1]
    face_above = faces_vertical[1:]
    face_left = jnp.concatenate([zero_col, faces_across], axis=1)
    face_right = jnp.concatenate([faces_across, zero_col], axis=1)
    face_front = jnp.concatenate([zero_lane, faces_along], axis=2)
    face_back = jnp.concatenate([faces_along, zero_lane], axis=2)
    diagonal = STORE + face_below + face_above + face_left + face_right + face_front + face_back
    coeffs = (diagonal, face_below, face_above, face_left, face_right, face_front, face_back)
    own = slice(tile_cols, 2 * tile_cols)
    own_coeffs = tuple(member[:, own] for member in coeffs)

    slab_index = lax.axis_index("sub")
    bounds = jnp.concatenate(
        [jnp.zeros((1,), jnp.int32), intersection_depth, jnp.zeros((1,), jnp.int32)]
    )
    depth_low = bounds[slab_index]
    depth_high = bounds[slab_index + 1]
    offsets = jnp.arange(margin_rows, dtype=jnp.int32) - OV
    inside_slab = (offsets >= -depth_low) & (offsets < slab_rows + depth_high)
    band_rows = (offsets < depth_low) | (offsets >= slab_rows - depth_high)
    active = jnp.where(inside_slab, 1.0, 0.0).reshape(margin_rows, 1, 1)
    weight = jnp.where(inside_slab & band_rows, 0.5, jnp.where(inside_slab, 1.0, 0.0)).reshape(
        margin_rows, 1, 1
    )
    full_active = jnp.broadcast_to(active, diagonal.shape)
    own_active = jnp.broadcast_to(active, own_coeffs[0].shape)
    factors_x = line_factors(own_coeffs, own_active, 1)
    factors_y = line_factors(coeffs, full_active, 2)
    factors_z = line_factors(coeffs, full_active, 0)

    rows_pad = jnp.zeros_like(pressure_wide[:1])
    for outer_turn in range(OUTER):
        center = pressure_wide[1:-1]
        coupled = (
            face_below * pressure_wide[:-2]
            + face_above * pressure_wide[2:]
            + face_left * lower_nb(center, 1)
            + face_right * upper_nb(center, 1)
            + face_front * lower_nb(center, 2)
            + face_back * upper_nb(center, 2)
        )
        residual = source_wide - (diagonal * center - coupled)
        target = residual * active
        estimate_own = relax_weight(0) * solve_lines(factors_x, target[:, own])
        for round_index in range(ROUNDS):
            estimate = with_sides(estimate_own, "grp", 1)
            last = round_index + 1 == ROUNDS
            estimate = round_call(
                relax_weight(round_index),
                0.0 if last else relax_weight(round_index + 1),
                last,
                tile_cols,
                estimate,
                target,
                coeffs,
                full_active,
                factors_y,
                factors_z,
                factors_x,
            )
            estimate_own = estimate
        correction = weight * estimate
        if outer_turn + 1 < OUTER:
            span = 2 * OV + 1
            from_below = lax.ppermute(
                correction[margin_rows - span :], "sub", grp_pairs("sub", 1)
            )
            from_above = lax.ppermute(correction[:span], "sub", grp_pairs("sub", -1))
            filler = jnp.zeros(
                (margin_rows + 2 - span,) + correction.shape[1:], jnp.float32
            )
            pressure_wide = (
                pressure_wide
                + jnp.concatenate([rows_pad, correction, rows_pad], axis=0)
                + jnp.concatenate([from_below, filler], axis=0)
                + jnp.concatenate([filler, from_above], axis=0)
            )
        else:
            own_corr = correction[:, own]
            from_below = lax.ppermute(
                own_corr[margin_rows - OV :], "sub", grp_pairs("sub", 1)
            )
            from_above = lax.ppermute(own_corr[:OV], "sub", grp_pairs("sub", -1))
            filler = jnp.zeros((slab_rows - OV, tile_cols, line_cells), jnp.float32)
            combined = (
                own_corr[OV : OV + slab_rows]
                + jnp.concatenate([from_below, filler], axis=0)
                + jnp.concatenate([filler, from_above], axis=0)
            )
            return pressure_wide[OV + 1 : OV + 1 + slab_rows, own] + combined


def solution(mesh):
    return jax.shard_map(
        on_device,
        mesh=mesh,
        in_specs=(
            P("sub", "grp", None),
            P(),
            P("sub", "grp", None),
            P("sub", "grp", None),
            P("sub", "grp", None),
            P(),
        ),
        out_specs=P("sub", "grp", None),
        check_vma=False,
    )
```

```python
import math

import jax
import jax.numpy as jnp
from jax import lax
from jax.sharding import PartitionSpec as P
from jax.experimental import pallas as pl
from jax.experimental.pallas import tpu as pltpu

OV = 4
BL = 8
ROUNDS = 4
OUTER = 2
FACIES = 8


STORE = 0.02


def relax_weight(round_index):
    return 1.0 / (1.4 + 0.6 * math.cos(math.pi * (2 * round_index + 1) / (2 * ROUNDS)))


def harmonic(former, second):
    inside = jnp.where((former > 0) & (second > 0), 1.0, 0.0)
    safe_former = jnp.where(former > 0, former, 1.0)
    safe_second = jnp.where(second > 0, second, 1.0)
    return inside * (2.0 * safe_former * safe_second / (safe_former + safe_second))


def lower_nb(field, axis, fill=0.0):
    extent = field.shape[axis]
    plane = jnp.full_like(lax.slice_in_dim(field, 0, 1, axis=axis), fill)
    return jnp.concatenate([plane, lax.slice_in_dim(field, 0, extent - 1, axis=axis)], axis=axis)


def upper_nb(field, axis, fill=0.0):
    extent = field.shape[axis]
    plane = jnp.full_like(lax.slice_in_dim(field, 0, 1, axis=axis), fill)
    return jnp.concatenate([lax.slice_in_dim(field, 1, extent, axis=axis), plane], axis=axis)


def apply_operator(coeffs, center):
    diagonal, face_below, face_above, face_left, face_right, face_front, face_back = coeffs
    coupled = (
        face_below * lower_nb(center, 0)
        + face_above * upper_nb(center, 0)
        + face_left * lower_nb(center, 1)
        + face_right * upper_nb(center, 1)
        + face_front * lower_nb(center, 2)
        + face_back * upper_nb(center, 2)
    )
    return diagonal * center - coupled


def block_position(shape, axis):
    broadcast_shape = [1] * len(shape)
    broadcast_shape[axis] = shape[axis]
    return (jnp.arange(shape[axis], dtype=jnp.int32) % BL).reshape(broadcast_shape)


def factor_lines(lower_band, middle, upper_band, axis):
    upper_prev = lower_nb(upper_band, axis)
    pivots = middle
    for _ in range(BL - 1):
        pivots = middle - (lower_band / lower_nb(pivots, axis, 1.0)) * upper_prev
    multipliers = lower_band / lower_nb(pivots, axis, 1.0)
    return (multipliers, 1.0 / pivots, upper_band, axis)


def solve_lines(factors, rhs):
    multipliers, inverse, upper_band, axis = factors
    forward = rhs
    for _ in range(BL - 1):
        forward = rhs - multipliers * lower_nb(forward, axis)
    result = forward * inverse
    for _ in range(BL - 1):
        result = (forward - upper_band * upper_nb(result, axis)) * inverse
    return result


def line_factors(coeffs, active, axis):
    diagonal = coeffs[0]
    line_axis = {0: 0, 1: 1, 2: 2}[axis]
    face_low = coeffs[2 * line_axis + 1]
    face_high = coeffs[2 * line_axis + 2]
    position = block_position(diagonal.shape, axis)
    if axis == 0:
        active_low = lower_nb(active, 0)
        active_high = upper_nb(active, 0)
    else:
        active_low = active
        active_high = active
    lower_band = jnp.where(position != 0, -face_low * active * active_low, 0.0)
    upper_band = jnp.where(position != BL - 1, -face_high * active * active_high, 0.0)
    middle = jnp.where(active > 0, diagonal, 1.0)
    return factor_lines(lower_band, middle, upper_band, axis)


def make_round_kernel(weight_now, weight_next, last, own_cols):
    def kernel(
        depth_ref, left_ref, own_ref, right_ref, t_ref, d_ref, fb_ref, fa_ref, fl_ref, fr_ref,
        ff_ref, fk_ref, ym_ref, yi_ref, zm_ref, zi_ref, xm_ref, xi_ref,
        o_ref, s_ref, f_ref, zu_ref,
    ):
        rows, cols, lanes = t_ref.shape
        shape = (rows, cols, lanes)
        offsets = lax.broadcasted_iota(jnp.int32, shape, 0) - OV
        slab_rows = rows - 2 * OV
        depth_low = depth_ref[0]
        depth_high = depth_ref[1]
        act = jnp.where(
            (offsets >= -depth_low) & (offsets < slab_rows + depth_high), 1.0, 0.0
        )
        act_high = jnp.where(
            (offsets + 1 >= -depth_low) & (offsets + 1 < slab_rows + depth_high) & (offsets + 1 < rows - OV),
            1.0,
            0.0,
        )
        lane_end = lax.broadcasted_iota(jnp.int32, shape, 2) % BL != BL - 1
        row_end = (offsets + OV) % BL != BL - 1
        zu_ref[...] = jnp.where(row_end, -fa_ref[...] * act * act_high, 0.0)

        def row_lower(x):
            return jnp.concatenate([jnp.zeros_like(x[:1]), x[:-1]], axis=0)

        def row_upper(x):
            return jnp.concatenate([x[1:], jnp.zeros_like(x[:1])], axis=0)

        def operate(e):
            coupled = (
                fb_ref[...] * row_lower(e)
                + fa_ref[...] * row_upper(e)
                + fl_ref[...] * pltpu.roll(e, 1, 1)
                + fr_ref[...] * pltpu.roll(e, cols - 1, 1)
                + ff_ref[...] * pltpu.roll(e, 1, 2)
                + fk_ref[...] * pltpu.roll(e, lanes - 1, 2)
            )
            return d_ref[...] * e - coupled

        def roll_solve(rhs, m, inv, u, axis, extent):
            forward = rhs
            for _ in range(BL - 1):
                forward = rhs - m * pltpu.roll(forward, 1, axis)
            result = forward * inv
            for _ in range(BL - 1):
                result = (forward - u * pltpu.roll(result, extent - 1, axis)) * inv
            return result

        target = t_ref[...]
        e = jnp.concatenate([left_ref[...], own_ref[...], right_ref[...]], axis=1)
        upper_y = jnp.where(lane_end, -fk_ref[...] * act * act, 0.0)
        update = act * (target - operate(e))
        e = e + weight_now * roll_solve(update, ym_ref[...], yi_ref[...], upper_y, 2, lanes)
        s_ref[...] = act * (target - operate(e))
        for block in range(rows // BL):
            base = block * BL
            forward = s_ref[base]
            f_ref[base] = forward
            for position in range(1, BL):
                r = base + position
                forward = s_ref[r] - zm_ref[r] * forward
                f_ref[r] = forward
            result = forward * zi_ref[base + BL - 1]
            s_ref[base + BL - 1] = result
            for position in range(BL - 2, -1, -1):
                r = base + position
                result = (f_ref[r] - zu_ref[r] * result) * zi_ref[r]
                s_ref[r] = result
        e = e + weight_now * s_ref[...]
        if last:
            o_ref[...] = e
        else:
            update = (act * (target - operate(e)))[:, own_cols]
            own_act = act[:, own_cols]
            col_end = lax.broadcasted_iota(jnp.int32, update.shape, 1) % BL != BL - 1
            upper_x = jnp.where(col_end, -fr_ref[:, own_cols] * own_act * own_act, 0.0)
            o_ref[...] = e[:, own_cols] + weight_next * roll_solve(
                update, xm_ref[...], xi_ref[...], upper_x, 1, BL
            )

    return kernel


def round_call(weight_now, weight_next, last, depths, pieces, target, coeffs, fy, fz, fx):
    tile_cols = pieces[1].shape[1]
    own_cols = slice(tile_cols, 2 * tile_cols)
    shape = target.shape
    out_shape = shape if last else pieces[1].shape
    vmem = pl.BlockSpec(memory_space=pltpu.VMEM)
    return pl.pallas_call(
        make_round_kernel(weight_now, weight_next, last, own_cols),
        out_shape=jax.ShapeDtypeStruct(out_shape, jnp.float32),
        in_specs=[pl.BlockSpec(memory_space=pltpu.SMEM)] + [vmem] * 17,
        out_specs=vmem,
        scratch_shapes=[pltpu.VMEM(shape, jnp.float32)] * 3,
    )(depths, *pieces, target, *coeffs, *fy[:2], *fz[:2], *fx[:2])


def grp_pairs(axis, by):
    devices = lax.axis_size(axis)
    return [(i, i + by) for i in range(devices) if 0 <= i + by < devices]


def with_sides(value, axis, dim):
    from_left = lax.ppermute(value, axis, grp_pairs(axis, 1))
    from_right = lax.ppermute(value, axis, grp_pairs(axis, -1))
    return jnp.concatenate([from_left, value, from_right], axis=dim)


def with_rows(value, axis, dim, width):
    length = value.shape[dim]
    below = lax.ppermute(
        lax.slice_in_dim(value, length - width, length, axis=dim), axis, grp_pairs(axis, 1)
    )
    above = lax.ppermute(lax.slice_in_dim(value, 0, width, axis=dim), axis, grp_pairs(axis, -1))
    return jnp.concatenate([below, value, above], axis=dim)


def with_halo(value, width):
    subs, grps = lax.axis_size("sub"), lax.axis_size("grp")
    top = value[:, -width:]
    bottom = value[:, :width]

    def diagonal(part, dsub, dgrp):
        pairs = [
            (s * grps + g, (s + dsub) * grps + g + dgrp)
            for s in range(subs)
            for g in range(grps)
            if 0 <= s + dsub < subs and 0 <= g + dgrp < grps
        ]
        return lax.ppermute(part, ("sub", "grp"), pairs)

    middle = jnp.concatenate(
        [
            lax.ppermute(top, "sub", grp_pairs("sub", 1)),
            value,
            lax.ppermute(bottom, "sub", grp_pairs("sub", -1)),
        ],
        axis=1,
    )
    left = jnp.concatenate(
        [
            diagonal(top, 1, 1),
            lax.ppermute(value, "grp", grp_pairs("grp", 1)),
            diagonal(bottom, -1, 1),
        ],
        axis=1,
    )
    right = jnp.concatenate(
        [
            diagonal(top, 1, -1),
            lax.ppermute(value, "grp", grp_pairs("grp", -1)),
            diagonal(bottom, -1, -1),
        ],
        axis=1,
    )
    return jnp.concatenate([left, middle, right], axis=2)


def on_device(facies, facies_perm, perm_scale, source, pressure_start, intersection_depth):
    slab_rows, tile_cols, line_cells = source.shape
    margin_rows = slab_rows + 2 * OV
    perm_local = jnp.zeros(source.shape, jnp.float32)
    for facies_kind in range(FACIES):
        perm_local = perm_local + jnp.where(facies == facies_kind, facies_perm[facies_kind], 0.0)
    perm_local = perm_local * perm_scale

    stacked = jnp.stack([perm_local, pressure_start, source])
    stacked = with_halo(stacked, OV + 1)
    perm_wide = stacked[0]
    pressure_wide = stacked[1]
    source_wide = stacked[2][1:-1]

    faces_vertical = harmonic(perm_wide[:-1], perm_wide[1:])
    middle_block = perm_wide[1:-1]
    faces_across = harmonic(middle_block[:, :-1], middle_block[:, 1:])
    faces_along = harmonic(middle_block[:, :, :-1], middle_block[:, :, 1:])
    zero_col = jnp.zeros_like(middle_block[:, :1])
    zero_lane = jnp.zeros_like(middle_block[:, :, :1])
    face_below = faces_vertical[:-1]
    face_above = faces_vertical[1:]
    face_left = jnp.concatenate([zero_col, faces_across], axis=1)
    face_right = jnp.concatenate([faces_across, zero_col], axis=1)
    face_front = jnp.concatenate([zero_lane, faces_along], axis=2)
    face_back = jnp.concatenate([faces_along, zero_lane], axis=2)
    diagonal = STORE + face_below + face_above + face_left + face_right + face_front + face_back
    coeffs = (diagonal, face_below, face_above, face_left, face_right, face_front, face_back)
    own = slice(tile_cols, 2 * tile_cols)
    own_coeffs = tuple(member[:, own] for member in coeffs)

    slab_index = lax.axis_index("sub")
    bounds = jnp.concatenate(
        [jnp.zeros((1,), jnp.int32), intersection_depth, jnp.zeros((1,), jnp.int32)]
    )
    depth_low = bounds[slab_index]
    depth_high = bounds[slab_index + 1]
    depths = jnp.stack([depth_low, depth_high])
    offsets = jnp.arange(margin_rows, dtype=jnp.int32) - OV
    inside_slab = (offsets >= -depth_low) & (offsets < slab_rows + depth_high)
    band_rows = (offsets < depth_low) | (offsets >= slab_rows - depth_high)
    active = jnp.where(inside_slab, 1.0, 0.0).reshape(margin_rows, 1, 1)
    weight = jnp.where(inside_slab & band_rows, 0.5, jnp.where(inside_slab, 1.0, 0.0)).reshape(
        margin_rows, 1, 1
    )
    full_active = jnp.broadcast_to(active, diagonal.shape)
    own_active = jnp.broadcast_to(active, own_coeffs[0].shape)
    factors_x = line_factors(own_coeffs, own_active, 1)
    factors_y = line_factors(coeffs, full_active, 2)
    factors_z = line_factors(coeffs, full_active, 0)

    rows_pad = jnp.zeros_like(pressure_wide[:1])
    for outer_turn in range(OUTER):
        center = pressure_wide[1:-1]
        coupled = (
            face_below * pressure_wide[:-2]
            + face_above * pressure_wide[2:]
            + face_left * lower_nb(center, 1)
            + face_right * upper_nb(center, 1)
            + face_front * lower_nb(center, 2)
            + face_back * upper_nb(center, 2)
        )
        residual = source_wide - (diagonal * center - coupled)
        target = residual * active
        estimate_own = relax_weight(0) * solve_lines(factors_x, target[:, own])
        for round_index in range(ROUNDS):
            pieces = (
                lax.ppermute(estimate_own, "grp", grp_pairs("grp", 1)),
                estimate_own,
                lax.ppermute(estimate_own, "grp", grp_pairs("grp", -1)),
            )
            last = round_index + 1 == ROUNDS
            estimate = round_call(
                relax_weight(round_index),
                0.0 if last else relax_weight(round_index + 1),
                last,
                depths,
                pieces,
                target,
                coeffs,
                factors_y,
                factors_z,
                factors_x,
            )
            estimate_own = estimate
        correction = weight * estimate
        if outer_turn + 1 < OUTER:
            span = 2 * OV + 1
            from_below = lax.ppermute(
                correction[margin_rows - span :], "sub", grp_pairs("sub", 1)
            )
            from_above = lax.ppermute(correction[:span], "sub", grp_pairs("sub", -1))
            filler = jnp.zeros(
                (margin_rows + 2 - span,) + correction.shape[1:], jnp.float32
            )
            pressure_wide = (
                pressure_wide
                + jnp.concatenate([rows_pad, correction, rows_pad], axis=0)
                + jnp.concatenate([from_below, filler], axis=0)
                + jnp.concatenate([filler, from_above], axis=0)
            )
        else:
            own_corr = correction[:, own]
            from_below = lax.ppermute(
                own_corr[margin_rows - OV :], "sub", grp_pairs("sub", 1)
            )
            from_above = lax.ppermute(own_corr[:OV], "sub", grp_pairs("sub", -1))
            filler = jnp.zeros((slab_rows - OV, tile_cols, line_cells), jnp.float32)
            combined = (
                own_corr[OV : OV + slab_rows]
                + jnp.concatenate([from_below, filler], axis=0)
                + jnp.concatenate([filler, from_above], axis=0)
            )
            return pressure_wide[OV + 1 : OV + 1 + slab_rows, own] + combined


def solution(mesh):
    return jax.shard_map(
        on_device,
        mesh=mesh,
        in_specs=(
            P("sub", "grp", None),
            P(),
            P("sub", "grp", None),
            P("sub", "grp", None),
            P("sub", "grp", None),
            P(),
        ),
        out_specs=P("sub", "grp", None),
        check_vma=False,
    )
```

```python
import math

import jax
import jax.numpy as jnp
from jax import lax
from jax.sharding import PartitionSpec as P
from jax.experimental import pallas as pl
from jax.experimental.pallas import tpu as pltpu

OV = 4
BL = 8
ROUNDS = 4
OUTER = 2
FACIES = 8


STORE = 0.02


def relax_weight(round_index):
    return 1.0 / (1.4 + 0.6 * math.cos(math.pi * (2 * round_index + 1) / (2 * ROUNDS)))


def harmonic(former, second):
    inside = jnp.where((former > 0) & (second > 0), 1.0, 0.0)
    safe_former = jnp.where(former > 0, former, 1.0)
    safe_second = jnp.where(second > 0, second, 1.0)
    return inside * (2.0 * safe_former * safe_second / (safe_former + safe_second))


def lower_nb(field, axis, fill=0.0):
    extent = field.shape[axis]
    plane = jnp.full_like(lax.slice_in_dim(field, 0, 1, axis=axis), fill)
    return jnp.concatenate([plane, lax.slice_in_dim(field, 0, extent - 1, axis=axis)], axis=axis)


def upper_nb(field, axis, fill=0.0):
    extent = field.shape[axis]
    plane = jnp.full_like(lax.slice_in_dim(field, 0, 1, axis=axis), fill)
    return jnp.concatenate([lax.slice_in_dim(field, 1, extent, axis=axis), plane], axis=axis)


def apply_operator(coeffs, center):
    diagonal, face_below, face_above, face_left, face_right, face_front, face_back = coeffs
    coupled = (
        face_below * lower_nb(center, 0)
        + face_above * upper_nb(center, 0)
        + face_left * lower_nb(center, 1)
        + face_right * upper_nb(center, 1)
        + face_front * lower_nb(center, 2)
        + face_back * upper_nb(center, 2)
    )
    return diagonal * center - coupled


def block_position(shape, axis):
    broadcast_shape = [1] * len(shape)
    broadcast_shape[axis] = shape[axis]
    return (jnp.arange(shape[axis], dtype=jnp.int32) % BL).reshape(broadcast_shape)


def factor_lines(lower_band, middle, upper_band, axis):
    upper_prev = lower_nb(upper_band, axis)
    pivots = middle
    for _ in range(BL - 1):
        pivots = middle - (lower_band / lower_nb(pivots, axis, 1.0)) * upper_prev
    multipliers = lower_band / lower_nb(pivots, axis, 1.0)
    return (multipliers, 1.0 / pivots, upper_band, axis)


def solve_lines(factors, rhs):
    multipliers, inverse, upper_band, axis = factors
    forward = rhs
    for _ in range(BL - 1):
        forward = rhs - multipliers * lower_nb(forward, axis)
    result = forward * inverse
    for _ in range(BL - 1):
        result = (forward - upper_band * upper_nb(result, axis)) * inverse
    return result


def line_factors(coeffs, active, axis):
    diagonal = coeffs[0]
    line_axis = {0: 0, 1: 1, 2: 2}[axis]
    face_low = coeffs[2 * line_axis + 1]
    face_high = coeffs[2 * line_axis + 2]
    position = block_position(diagonal.shape, axis)
    if axis == 0:
        active_low = lower_nb(active, 0)
        active_high = upper_nb(active, 0)
    else:
        active_low = active
        active_high = active
    lower_band = jnp.where(position != 0, -face_low * active * active_low, 0.0)
    upper_band = jnp.where(position != BL - 1, -face_high * active * active_high, 0.0)
    middle = jnp.where(active > 0, diagonal, 1.0)
    return factor_lines(lower_band, middle, upper_band, axis)


def make_round_kernel(weight_now, weight_next, last, own_cols):
    def kernel(
        depth_ref, left_ref, own_ref, right_ref, t_ref, d_ref, fb_ref, fa_ref, fl_ref, fr_ref,
        ff_ref, fk_ref, ym_ref, yi_ref, zm_ref, zi_ref, xm_ref, xi_ref,
        o_ref, s_ref, f_ref, zu_ref,
    ):
        rows, cols, lanes = t_ref.shape
        shape = (rows, cols, lanes)
        offsets = lax.broadcasted_iota(jnp.int32, shape, 0) - OV
        slab_rows = rows - 2 * OV
        depth_low = depth_ref[0]
        depth_high = depth_ref[1]
        act = jnp.where(
            (offsets >= -depth_low) & (offsets < slab_rows + depth_high), 1.0, 0.0
        )
        act_high = jnp.where(
            (offsets + 1 >= -depth_low) & (offsets + 1 < slab_rows + depth_high) & (offsets + 1 < rows - OV),
            1.0,
            0.0,
        )
        lane_end = lax.broadcasted_iota(jnp.int32, shape, 2) % BL != BL - 1
        row_end = (offsets + OV) % BL != BL - 1
        zu_ref[...] = jnp.where(row_end, -fa_ref[...] * act * act_high, 0.0)

        def row_lower(x):
            return jnp.concatenate([jnp.zeros_like(x[:1]), x[:-1]], axis=0)

        def row_upper(x):
            return jnp.concatenate([x[1:], jnp.zeros_like(x[:1])], axis=0)

        def operate(e):
            coupled = (
                fb_ref[...] * row_lower(e)
                + fa_ref[...] * row_upper(e)
                + fl_ref[...] * pltpu.roll(e, 1, 1)
                + fr_ref[...] * pltpu.roll(e, cols - 1, 1)
                + ff_ref[...] * pltpu.roll(e, 1, 2)
                + fk_ref[...] * pltpu.roll(e, lanes - 1, 2)
            )
            return d_ref[...] * e - coupled

        def roll_solve(rhs, m, inv, u, axis, extent):
            forward = rhs
            for _ in range(BL - 1):
                forward = rhs - m * pltpu.roll(forward, 1, axis)
            result = forward * inv
            for _ in range(BL - 1):
                result = (forward - u * pltpu.roll(result, extent - 1, axis)) * inv
            return result

        target = t_ref[...]
        e = jnp.concatenate([left_ref[...], own_ref[...], right_ref[...]], axis=1)
        upper_y = jnp.where(lane_end, -fk_ref[...] * act * act, 0.0)
        update = act * (target - operate(e))
        e = e + weight_now * roll_solve(update, ym_ref[...], yi_ref[...], upper_y, 2, lanes)
        s_ref[...] = act * (target - operate(e))
        for block in range(rows // BL):
            base = block * BL
            forward = s_ref[base]
            f_ref[base] = forward
            for position in range(1, BL):
                r = base + position
                forward = s_ref[r] - zm_ref[r] * forward
                f_ref[r] = forward
            result = forward * zi_ref[base + BL - 1]
            s_ref[base + BL - 1] = result
            for position in range(BL - 2, -1, -1):
                r = base + position
                result = (f_ref[r] - zu_ref[r] * result) * zi_ref[r]
                s_ref[r] = result
        e = e + weight_now * s_ref[...]
        if last:
            o_ref[...] = e
        else:
            update = (act * (target - operate(e)))[:, own_cols]
            own_act = act[:, own_cols]
            col_end = lax.broadcasted_iota(jnp.int32, update.shape, 1) % BL != BL - 1
            upper_x = jnp.where(col_end, -fr_ref[:, own_cols] * own_act * own_act, 0.0)
            o_ref[...] = e[:, own_cols] + weight_next * roll_solve(
                update, xm_ref[...], xi_ref[...], upper_x, 1, BL
            )

    return kernel


def round_call(weight_now, weight_next, last, depths, pieces, target, coeffs, fy, fz, fx):
    tile_cols = pieces[1].shape[1]
    own_cols = slice(tile_cols, 2 * tile_cols)
    shape = target.shape
    out_shape = shape if last else pieces[1].shape
    vmem = pl.BlockSpec(memory_space=pltpu.VMEM)
    return pl.pallas_call(
        make_round_kernel(weight_now, weight_next, last, own_cols),
        out_shape=jax.ShapeDtypeStruct(out_shape, jnp.float32),
        in_specs=[pl.BlockSpec(memory_space=pltpu.SMEM)] + [vmem] * 17,
        out_specs=vmem,
        scratch_shapes=[pltpu.VMEM(shape, jnp.float32)] * 3,
    )(depths, *pieces, target, *coeffs, *fy[:2], *fz[:2], *fx[:2])


def grp_pairs(axis, by):
    devices = lax.axis_size(axis)
    return [(i, i + by) for i in range(devices) if 0 <= i + by < devices]


def with_sides(value, axis, dim):
    from_left = lax.ppermute(value, axis, grp_pairs(axis, 1))
    from_right = lax.ppermute(value, axis, grp_pairs(axis, -1))
    return jnp.concatenate([from_left, value, from_right], axis=dim)


def with_rows(value, axis, dim, width):
    length = value.shape[dim]
    below = lax.ppermute(
        lax.slice_in_dim(value, length - width, length, axis=dim), axis, grp_pairs(axis, 1)
    )
    above = lax.ppermute(lax.slice_in_dim(value, 0, width, axis=dim), axis, grp_pairs(axis, -1))
    return jnp.concatenate([below, value, above], axis=dim)


def with_halo(value, width):
    subs, grps = lax.axis_size("sub"), lax.axis_size("grp")
    top = value[:, -width:]
    bottom = value[:, :width]

    def diagonal(part, dsub, dgrp):
        pairs = [
            (s * grps + g, (s + dsub) * grps + g + dgrp)
            for s in range(subs)
            for g in range(grps)
            if 0 <= s + dsub < subs and 0 <= g + dgrp < grps
        ]
        return lax.ppermute(part, ("sub", "grp"), pairs)

    middle = jnp.concatenate(
        [
            lax.ppermute(top, "sub", grp_pairs("sub", 1)),
            value,
            lax.ppermute(bottom, "sub", grp_pairs("sub", -1)),
        ],
        axis=1,
    )
    left = jnp.concatenate(
        [
            diagonal(top, 1, 1),
            lax.ppermute(value, "grp", grp_pairs("grp", 1)),
            diagonal(bottom, -1, 1),
        ],
        axis=1,
    )
    right = jnp.concatenate(
        [
            diagonal(top, 1, -1),
            lax.ppermute(value, "grp", grp_pairs("grp", -1)),
            diagonal(bottom, -1, -1),
        ],
        axis=1,
    )
    return jnp.concatenate([left, middle, right], axis=2)


def on_device(facies, facies_perm, perm_scale, source, pressure_start, intersection_depth):
    slab_rows, tile_cols, line_cells = source.shape
    margin_rows = slab_rows + 2 * OV
    perm_local = jnp.zeros(source.shape, jnp.float32)
    for facies_kind in range(FACIES):
        perm_local = perm_local + jnp.where(facies == facies_kind, facies_perm[facies_kind], 0.0)
    perm_local = perm_local * perm_scale

    stacked = jnp.stack([perm_local, pressure_start, source])
    stacked = with_rows(stacked, "sub", 1, OV + 1)
    stacked = with_sides(stacked, "grp", 2)
    perm_wide = stacked[0]
    pressure_wide = stacked[1]
    source_wide = stacked[2][1:-1]

    faces_vertical = harmonic(perm_wide[:-1], perm_wide[1:])
    middle_block = perm_wide[1:-1]
    faces_across = harmonic(middle_block[:, :-1], middle_block[:, 1:])
    faces_along = harmonic(middle_block[:, :, :-1], middle_block[:, :, 1:])
    zero_col = jnp.zeros_like(middle_block[:, :1])
    zero_lane = jnp.zeros_like(middle_block[:, :, :1])
    face_below = faces_vertical[:-1]
    face_above = faces_vertical[1:]
    face_left = jnp.concatenate([zero_col, faces_across], axis=1)
    face_right = jnp.concatenate([faces_across, zero_col], axis=1)
    face_front = jnp.concatenate([zero_lane, faces_along], axis=2)
    face_back = jnp.concatenate([faces_along, zero_lane], axis=2)
    diagonal = STORE + face_below + face_above + face_left + face_right + face_front + face_back
    coeffs = (diagonal, face_below, face_above, face_left, face_right, face_front, face_back)
    own = slice(tile_cols, 2 * tile_cols)
    own_coeffs = tuple(member[:, own] for member in coeffs)

    slab_index = lax.axis_index("sub")
    bounds = jnp.concatenate(
        [jnp.zeros((1,), jnp.int32), intersection_depth, jnp.zeros((1,), jnp.int32)]
    )
    depth_low = bounds[slab_index]
    depth_high = bounds[slab_index + 1]
    depths = jnp.stack([depth_low, depth_high])
    offsets = jnp.arange(margin_rows, dtype=jnp.int32) - OV
    inside_slab = (offsets >= -depth_low) & (offsets < slab_rows + depth_high)
    band_rows = (offsets < depth_low) | (offsets >= slab_rows - depth_high)
    active = jnp.where(inside_slab, 1.0, 0.0).reshape(margin_rows, 1, 1)
    weight = jnp.where(inside_slab & band_rows, 0.5, jnp.where(inside_slab, 1.0, 0.0)).reshape(
        margin_rows, 1, 1
    )
    full_active = jnp.broadcast_to(active, diagonal.shape)
    own_active = jnp.broadcast_to(active, own_coeffs[0].shape)
    factors_x = line_factors(own_coeffs, own_active, 1)
    factors_y = line_factors(coeffs, full_active, 2)
    factors_z = line_factors(coeffs, full_active, 0)

    rows_pad = jnp.zeros_like(pressure_wide[:1])
    for outer_turn in range(OUTER):
        center = pressure_wide[1:-1]
        coupled = (
            face_below * pressure_wide[:-2]
            + face_above * pressure_wide[2:]
            + face_left * lower_nb(center, 1)
            + face_right * upper_nb(center, 1)
            + face_front * lower_nb(center, 2)
            + face_back * upper_nb(center, 2)
        )
        residual = source_wide - (diagonal * center - coupled)
        target = residual * active
        estimate_own = relax_weight(0) * solve_lines(factors_x, target[:, own])
        for round_index in range(ROUNDS):
            pieces = (
                lax.ppermute(estimate_own, "grp", grp_pairs("grp", 1)),
                estimate_own,
                lax.ppermute(estimate_own, "grp", grp_pairs("grp", -1)),
            )
            last = round_index + 1 == ROUNDS
            estimate = round_call(
                relax_weight(round_index),
                0.0 if last else relax_weight(round_index + 1),
                last,
                depths,
                pieces,
                target,
                coeffs,
                factors_y,
                factors_z,
                factors_x,
            )
            estimate_own = estimate
        correction = weight * estimate
        if outer_turn + 1 < OUTER:
            span = 2 * OV + 1
            from_below = lax.ppermute(
                correction[margin_rows - span :], "sub", grp_pairs("sub", 1)
            )
            from_above = lax.ppermute(correction[:span], "sub", grp_pairs("sub", -1))
            filler = jnp.zeros(
                (margin_rows + 2 - span,) + correction.shape[1:], jnp.float32
            )
            pressure_wide = (
                pressure_wide
                + jnp.concatenate([rows_pad, correction, rows_pad], axis=0)
                + jnp.concatenate([from_below, filler], axis=0)
                + jnp.concatenate([filler, from_above], axis=0)
            )
        else:
            own_corr = correction[:, own]
            from_below = lax.ppermute(
                own_corr[margin_rows - OV :], "sub", grp_pairs("sub", 1)
            )
            from_above = lax.ppermute(own_corr[:OV], "sub", grp_pairs("sub", -1))
            filler = jnp.zeros((slab_rows - OV, tile_cols, line_cells), jnp.float32)
            combined = (
                own_corr[OV : OV + slab_rows]
                + jnp.concatenate([from_below, filler], axis=0)
                + jnp.concatenate([filler, from_above], axis=0)
            )
            return pressure_wide[OV + 1 : OV + 1 + slab_rows, own] + combined


def solution(mesh):
    return jax.shard_map(
        on_device,
        mesh=mesh,
        in_specs=(
            P("sub", "grp", None),
            P(),
            P("sub", "grp", None),
            P("sub", "grp", None),
            P("sub", "grp", None),
            P(),
        ),
        out_specs=P("sub", "grp", None),
        check_vma=False,
    )
```

```python
import math

import jax
import jax.numpy as jnp
from jax import lax
from jax.sharding import PartitionSpec as P
from jax.experimental import pallas as pl
from jax.experimental.pallas import tpu as pltpu

OV = 4
BL = 8
ROUNDS = 4
OUTER = 2
FACIES = 8


STORE = 0.02


def relax_weight(round_index):
    return 1.0 / (1.4 + 0.6 * math.cos(math.pi * (2 * round_index + 1) / (2 * ROUNDS)))


def harmonic(former, second):
    inside = jnp.where((former > 0) & (second > 0), 1.0, 0.0)
    safe_former = jnp.where(former > 0, former, 1.0)
    safe_second = jnp.where(second > 0, second, 1.0)
    return inside * (2.0 * safe_former * safe_second / (safe_former + safe_second))


def lower_nb(field, axis, fill=0.0):
    extent = field.shape[axis]
    plane = jnp.full_like(lax.slice_in_dim(field, 0, 1, axis=axis), fill)
    return jnp.concatenate([plane, lax.slice_in_dim(field, 0, extent - 1, axis=axis)], axis=axis)


def upper_nb(field, axis, fill=0.0):
    extent = field.shape[axis]
    plane = jnp.full_like(lax.slice_in_dim(field, 0, 1, axis=axis), fill)
    return jnp.concatenate([lax.slice_in_dim(field, 1, extent, axis=axis), plane], axis=axis)


def apply_operator(coeffs, center):
    diagonal, face_below, face_above, face_left, face_right, face_front, face_back = coeffs
    coupled = (
        face_below * lower_nb(center, 0)
        + face_above * upper_nb(center, 0)
        + face_left * lower_nb(center, 1)
        + face_right * upper_nb(center, 1)
        + face_front * lower_nb(center, 2)
        + face_back * upper_nb(center, 2)
    )
    return diagonal * center - coupled


def block_position(shape, axis):
    broadcast_shape = [1] * len(shape)
    broadcast_shape[axis] = shape[axis]
    return (jnp.arange(shape[axis], dtype=jnp.int32) % BL).reshape(broadcast_shape)


def factor_lines(lower_band, middle, upper_band, axis):
    upper_prev = lower_nb(upper_band, axis)
    pivots = middle
    for _ in range(BL - 1):
        pivots = middle - (lower_band / lower_nb(pivots, axis, 1.0)) * upper_prev
    multipliers = lower_band / lower_nb(pivots, axis, 1.0)
    return (multipliers, 1.0 / pivots, upper_band, axis)


def solve_lines(factors, rhs):
    multipliers, inverse, upper_band, axis = factors
    forward = rhs
    for _ in range(BL - 1):
        forward = rhs - multipliers * lower_nb(forward, axis)
    result = forward * inverse
    for _ in range(BL - 1):
        result = (forward - upper_band * upper_nb(result, axis)) * inverse
    return result


def line_factors(coeffs, active, axis):
    diagonal = coeffs[0]
    line_axis = {0: 0, 1: 1, 2: 2}[axis]
    face_low = coeffs[2 * line_axis + 1]
    face_high = coeffs[2 * line_axis + 2]
    position = block_position(diagonal.shape, axis)
    if axis == 0:
        active_low = lower_nb(active, 0)
        active_high = upper_nb(active, 0)
    else:
        active_low = active
        active_high = active
    lower_band = jnp.where(position != 0, -face_low * active * active_low, 0.0)
    upper_band = jnp.where(position != BL - 1, -face_high * active * active_high, 0.0)
    middle = jnp.where(active > 0, diagonal, 1.0)
    return factor_lines(lower_band, middle, upper_band, axis)


def make_round_kernel(weight_now, weight_next, last, own_cols):
    def kernel(
        depth_ref, left_ref, own_ref, right_ref, t_ref, d_ref, fb_ref, fa_ref, fl_ref, fr_ref,
        ff_ref, fk_ref, ym_ref, yi_ref, zm_ref, zi_ref, xm_ref, xi_ref,
        o_ref, s_ref, f_ref, zu_ref,
    ):
        rows, cols, lanes = t_ref.shape
        shape = (rows, cols, lanes)
        offsets = lax.broadcasted_iota(jnp.int32, shape, 0) - OV
        slab_rows = rows - 2 * OV
        depth_low = depth_ref[0]
        depth_high = depth_ref[1]
        act = jnp.where(
            (offsets >= -depth_low) & (offsets < slab_rows + depth_high), 1.0, 0.0
        )
        act_high = jnp.where(
            (offsets + 1 >= -depth_low) & (offsets + 1 < slab_rows + depth_high) & (offsets + 1 < rows - OV),
            1.0,
            0.0,
        )
        lane_end = lax.broadcasted_iota(jnp.int32, shape, 2) % BL != BL - 1
        row_end = (offsets + OV) % BL != BL - 1
        zu_ref[...] = jnp.where(row_end, -fa_ref[...] * act * act_high, 0.0)

        def row_lower(x):
            return jnp.concatenate([jnp.zeros_like(x[:1]), x[:-1]], axis=0)

        def row_upper(x):
            return jnp.concatenate([x[1:], jnp.zeros_like(x[:1])], axis=0)

        def operate(e):
            coupled = (
                fb_ref[...] * row_lower(e)
                + fa_ref[...] * row_upper(e)
                + fl_ref[...] * pltpu.roll(e, 1, 1)
                + fr_ref[...] * pltpu.roll(e, cols - 1, 1)
                + ff_ref[...] * pltpu.roll(e, 1, 2)
                + fk_ref[...] * pltpu.roll(e, lanes - 1, 2)
            )
            return d_ref[...] * e - coupled

        def roll_solve(rhs, m, inv, u, axis, extent):
            forward = rhs
            for _ in range(BL - 1):
                forward = rhs - m * pltpu.roll(forward, 1, axis)
            result = forward * inv
            for _ in range(BL - 1):
                result = (forward - u * pltpu.roll(result, extent - 1, axis)) * inv
            return result

        target = t_ref[...]
        e = jnp.concatenate([left_ref[...], own_ref[...], right_ref[...]], axis=1)
        upper_y = jnp.where(lane_end, -fk_ref[...] * act * act, 0.0)
        update = act * (target - operate(e))
        e = e + weight_now * roll_solve(update, ym_ref[...], yi_ref[...], upper_y, 2, lanes)
        s_ref[...] = act * (target - operate(e))
        for block in range(rows // BL):
            base = block * BL
            forward = s_ref[base]
            f_ref[base] = forward
            for position in range(1, BL):
                r = base + position
                forward = s_ref[r] - zm_ref[r] * forward
                f_ref[r] = forward
            result = forward * zi_ref[base + BL - 1]
            s_ref[base + BL - 1] = result
            for position in range(BL - 2, -1, -1):
                r = base + position
                result = (f_ref[r] - zu_ref[r] * result) * zi_ref[r]
                s_ref[r] = result
        e = e + weight_now * s_ref[...]
        if last:
            o_ref[...] = e
        else:
            update = (act * (target - operate(e)))[:, own_cols]
            own_act = act[:, own_cols]
            col_end = lax.broadcasted_iota(jnp.int32, update.shape, 1) % BL != BL - 1
            upper_x = jnp.where(col_end, -fr_ref[:, own_cols] * own_act * own_act, 0.0)
            o_ref[...] = e[:, own_cols] + weight_next * roll_solve(
                update, xm_ref[...], xi_ref[...], upper_x, 1, BL
            )

    return kernel


def round_call(weight_now, weight_next, last, depths, pieces, target, coeffs, fy, fz, fx):
    tile_cols = pieces[1].shape[1]
    own_cols = slice(tile_cols, 2 * tile_cols)
    shape = target.shape
    out_shape = shape if last else pieces[1].shape
    vmem = pl.BlockSpec(memory_space=pltpu.VMEM)
    return pl.pallas_call(
        make_round_kernel(weight_now, weight_next, last, own_cols),
        out_shape=jax.ShapeDtypeStruct(out_shape, jnp.float32),
        in_specs=[pl.BlockSpec(memory_space=pltpu.SMEM)] + [vmem] * 17,
        out_specs=vmem,
        scratch_shapes=[pltpu.VMEM(shape, jnp.float32)] * 3,
    )(depths, *pieces, target, *coeffs, *fy[:2], *fz[:2], *fx[:2])


def grp_pairs(axis, by):
    devices = lax.axis_size(axis)
    return [(i, i + by) for i in range(devices) if 0 <= i + by < devices]


def with_sides(value, axis, dim):
    from_left = lax.ppermute(value, axis, grp_pairs(axis, 1))
    from_right = lax.ppermute(value, axis, grp_pairs(axis, -1))
    return jnp.concatenate([from_left, value, from_right], axis=dim)


def with_rows(value, axis, dim, width):
    length = value.shape[dim]
    below = lax.ppermute(
        lax.slice_in_dim(value, length - width, length, axis=dim), axis, grp_pairs(axis, 1)
    )
    above = lax.ppermute(lax.slice_in_dim(value, 0, width, axis=dim), axis, grp_pairs(axis, -1))
    return jnp.concatenate([below, value, above], axis=dim)


def with_halo(value, width):
    subs, grps = lax.axis_size("sub"), lax.axis_size("grp")
    top = value[:, -width:]
    bottom = value[:, :width]

    def diagonal(part, dsub, dgrp):
        pairs = [
            (s * grps + g, (s + dsub) * grps + g + dgrp)
            for s in range(subs)
            for g in range(grps)
            if 0 <= s + dsub < subs and 0 <= g + dgrp < grps
        ]
        return lax.ppermute(part, ("sub", "grp"), pairs)

    middle = jnp.concatenate(
        [
            lax.ppermute(top, "sub", grp_pairs("sub", 1)),
            value,
            lax.ppermute(bottom, "sub", grp_pairs("sub", -1)),
        ],
        axis=1,
    )
    left = jnp.concatenate(
        [
            diagonal(top, 1, 1),
            lax.ppermute(value, "grp", grp_pairs("grp", 1)),
            diagonal(bottom, -1, 1),
        ],
        axis=1,
    )
    right = jnp.concatenate(
        [
            diagonal(top, 1, -1),
            lax.ppermute(value, "grp", grp_pairs("grp", -1)),
            diagonal(bottom, -1, -1),
        ],
        axis=1,
    )
    return jnp.concatenate([left, middle, right], axis=2)


def on_device(facies, facies_perm, perm_scale, source, pressure_start, intersection_depth):
    slab_rows, tile_cols, line_cells = source.shape
    margin_rows = slab_rows + 2 * OV
    perm_local = jnp.zeros(source.shape, jnp.float32)
    for facies_kind in range(FACIES):
        perm_local = perm_local + jnp.where(facies == facies_kind, facies_perm[facies_kind], 0.0)
    perm_local = perm_local * perm_scale

    stacked = jnp.stack([perm_local, pressure_start, source])
    stacked = with_rows(stacked, "sub", 1, OV + 1)
    far_left = lax.ppermute(stacked[:, :, tile_cols - 1 :], "grp", grp_pairs("grp", 2))
    far_right = lax.ppermute(stacked[:, :, :1], "grp", grp_pairs("grp", -2))
    stacked = with_sides(stacked, "grp", 2)
    pressure_edge = jnp.concatenate([far_left[1], stacked[1], far_right[1]], axis=1)
    perm_edge = jnp.concatenate([far_left[0], stacked[0], far_right[0]], axis=1)
    perm_wide = stacked[0]
    pressure_wide = stacked[1]
    source_wide = stacked[2][1:-1]

    faces_vertical = harmonic(perm_wide[:-1], perm_wide[1:])
    middle_block = perm_wide[1:-1]
    middle_edge = perm_edge[1:-1]
    faces_across = harmonic(middle_edge[:, :-1], middle_edge[:, 1:])
    faces_along = harmonic(middle_block[:, :, :-1], middle_block[:, :, 1:])
    zero_lane = jnp.zeros_like(middle_block[:, :, :1])
    face_below = faces_vertical[:-1]
    face_above = faces_vertical[1:]
    face_left = faces_across[:, :-1]
    face_right = faces_across[:, 1:]
    face_front = jnp.concatenate([zero_lane, faces_along], axis=2)
    face_back = jnp.concatenate([faces_along, zero_lane], axis=2)
    diagonal = STORE + face_below + face_above + face_left + face_right + face_front + face_back
    coeffs = (diagonal, face_below, face_above, face_left, face_right, face_front, face_back)
    own = slice(tile_cols, 2 * tile_cols)
    own_coeffs = tuple(member[:, own] for member in coeffs)

    slab_index = lax.axis_index("sub")
    bounds = jnp.concatenate(
        [jnp.zeros((1,), jnp.int32), intersection_depth, jnp.zeros((1,), jnp.int32)]
    )
    depth_low = bounds[slab_index]
    depth_high = bounds[slab_index + 1]
    depths = jnp.stack([depth_low, depth_high])
    offsets = jnp.arange(margin_rows, dtype=jnp.int32) - OV
    inside_slab = (offsets >= -depth_low) & (offsets < slab_rows + depth_high)
    band_rows = (offsets < depth_low) | (offsets >= slab_rows - depth_high)
    active = jnp.where(inside_slab, 1.0, 0.0).reshape(margin_rows, 1, 1)
    weight = jnp.where(inside_slab & band_rows, 0.5, jnp.where(inside_slab, 1.0, 0.0)).reshape(
        margin_rows, 1, 1
    )
    full_active = jnp.broadcast_to(active, diagonal.shape)
    own_active = jnp.broadcast_to(active, own_coeffs[0].shape)
    factors_x = line_factors(own_coeffs, own_active, 1)
    factors_wide_x = line_factors(coeffs, full_active, 1)
    factors_y = line_factors(coeffs, full_active, 2)
    factors_z = line_factors(coeffs, full_active, 0)

    rows_pad = jnp.zeros_like(pressure_wide[:1])
    for outer_turn in range(OUTER):
        if outer_turn > 0:
            pressure_edge = jnp.pad(pressure_wide, ((0, 0), (1, 1), (0, 0)))
        center = pressure_wide[1:-1]
        coupled = (
            face_below * pressure_wide[:-2]
            + face_above * pressure_wide[2:]
            + face_left * pressure_edge[1:-1, :-2]
            + face_right * pressure_edge[1:-1, 2:]
            + face_front * lower_nb(center, 2)
            + face_back * upper_nb(center, 2)
        )
        residual = source_wide - (diagonal * center - coupled)
        target = residual * active
        if outer_turn == 0:
            first = relax_weight(0) * solve_lines(factors_wide_x, target)
            first_pieces = (first[:, :tile_cols], first[:, own], first[:, 2 * tile_cols :])
        else:
            estimate_own = relax_weight(0) * solve_lines(factors_x, target[:, own])
        for round_index in range(ROUNDS):
            if round_index == 0 and outer_turn == 0:
                pieces = first_pieces
            else:
                pieces = (
                    lax.ppermute(estimate_own, "grp", grp_pairs("grp", 1)),
                    estimate_own,
                    lax.ppermute(estimate_own, "grp", grp_pairs("grp", -1)),
                )
            last = round_index + 1 == ROUNDS
            estimate = round_call(
                relax_weight(round_index),
                0.0 if last else relax_weight(round_index + 1),
                last,
                depths,
                pieces,
                target,
                coeffs,
                factors_y,
                factors_z,
                factors_x,
            )
            estimate_own = estimate
        correction = weight * estimate
        if outer_turn + 1 < OUTER:
            span = 2 * OV + 1
            from_below = lax.ppermute(
                correction[margin_rows - span :], "sub", grp_pairs("sub", 1)
            )
            from_above = lax.ppermute(correction[:span], "sub", grp_pairs("sub", -1))
            filler = jnp.zeros(
                (margin_rows + 2 - span,) + correction.shape[1:], jnp.float32
            )
            pressure_wide = (
                pressure_wide
                + jnp.concatenate([rows_pad, correction, rows_pad], axis=0)
                + jnp.concatenate([from_below, filler], axis=0)
                + jnp.concatenate([filler, from_above], axis=0)
            )
        else:
            own_corr = correction[:, own]
            from_below = lax.ppermute(
                own_corr[margin_rows - OV :], "sub", grp_pairs("sub", 1)
            )
            from_above = lax.ppermute(own_corr[:OV], "sub", grp_pairs("sub", -1))
            filler = jnp.zeros((slab_rows - OV, tile_cols, line_cells), jnp.float32)
            combined = (
                own_corr[OV : OV + slab_rows]
                + jnp.concatenate([from_below, filler], axis=0)
                + jnp.concatenate([filler, from_above], axis=0)
            )
            return pressure_wide[OV + 1 : OV + 1 + slab_rows, own] + combined


def solution(mesh):
    return jax.shard_map(
        on_device,
        mesh=mesh,
        in_specs=(
            P("sub", "grp", None),
            P(),
            P("sub", "grp", None),
            P("sub", "grp", None),
            P("sub", "grp", None),
            P(),
        ),
        out_specs=P("sub", "grp", None),
        check_vma=False,
    )
```

```python
import math

import jax
import jax.numpy as jnp
from jax import lax
from jax.sharding import PartitionSpec as P
from jax.experimental import pallas as pl
from jax.experimental.pallas import tpu as pltpu

OV = 4
BL = 8
ROUNDS = 4
OUTER = 2
FACIES = 8


STORE = 0.02


def relax_weight(round_index):
    return 1.0 / (1.4 + 0.6 * math.cos(math.pi * (2 * round_index + 1) / (2 * ROUNDS)))


def harmonic(former, second):
    inside = jnp.where((former > 0) & (second > 0), 1.0, 0.0)
    safe_former = jnp.where(former > 0, former, 1.0)
    safe_second = jnp.where(second > 0, second, 1.0)
    return inside * (2.0 * safe_former * safe_second / (safe_former + safe_second))


def lower_nb(field, axis, fill=0.0):
    extent = field.shape[axis]
    plane = jnp.full_like(lax.slice_in_dim(field, 0, 1, axis=axis), fill)
    return jnp.concatenate([plane, lax.slice_in_dim(field, 0, extent - 1, axis=axis)], axis=axis)


def upper_nb(field, axis, fill=0.0):
    extent = field.shape[axis]
    plane = jnp.full_like(lax.slice_in_dim(field, 0, 1, axis=axis), fill)
    return jnp.concatenate([lax.slice_in_dim(field, 1, extent, axis=axis), plane], axis=axis)


def apply_operator(coeffs, center):
    diagonal, face_below, face_above, face_left, face_right, face_front, face_back = coeffs
    coupled = (
        face_below * lower_nb(center, 0)
        + face_above * upper_nb(center, 0)
        + face_left * lower_nb(center, 1)
        + face_right * upper_nb(center, 1)
        + face_front * lower_nb(center, 2)
        + face_back * upper_nb(center, 2)
    )
    return diagonal * center - coupled


def block_position(shape, axis):
    broadcast_shape = [1] * len(shape)
    broadcast_shape[axis] = shape[axis]
    return (jnp.arange(shape[axis], dtype=jnp.int32) % BL).reshape(broadcast_shape)


def factor_lines(lower_band, middle, upper_band, axis):
    upper_prev = lower_nb(upper_band, axis)
    pivots = middle
    for _ in range(BL - 1):
        pivots = middle - (lower_band / lower_nb(pivots, axis, 1.0)) * upper_prev
    multipliers = lower_band / lower_nb(pivots, axis, 1.0)
    return (multipliers, 1.0 / pivots, upper_band, axis)


def solve_lines(factors, rhs):
    multipliers, inverse, upper_band, axis = factors
    forward = rhs
    for _ in range(BL - 1):
        forward = rhs - multipliers * lower_nb(forward, axis)
    result = forward * inverse
    for _ in range(BL - 1):
        result = (forward - upper_band * upper_nb(result, axis)) * inverse
    return result


def line_factors(coeffs, active, axis):
    diagonal = coeffs[0]
    line_axis = {0: 0, 1: 1, 2: 2}[axis]
    face_low = coeffs[2 * line_axis + 1]
    face_high = coeffs[2 * line_axis + 2]
    position = block_position(diagonal.shape, axis)
    if axis == 0:
        active_low = lower_nb(active, 0)
        active_high = upper_nb(active, 0)
    else:
        active_low = active
        active_high = active
    lower_band = jnp.where(position != 0, -face_low * active * active_low, 0.0)
    upper_band = jnp.where(position != BL - 1, -face_high * active * active_high, 0.0)
    middle = jnp.where(active > 0, diagonal, 1.0)
    return factor_lines(lower_band, middle, upper_band, axis)


def make_round_kernel(weight_now, weight_next, last, own_cols):
    def kernel(
        depth_ref, left_ref, own_ref, right_ref, t_ref, d_ref, fb_ref, fa_ref, fl_ref, fr_ref,
        ff_ref, fk_ref, ym_ref, yi_ref, zm_ref, zi_ref, xm_ref, xi_ref,
        o_ref, s_ref, f_ref, zu_ref,
    ):
        rows, cols, lanes = t_ref.shape
        shape = (rows, cols, lanes)
        offsets = lax.broadcasted_iota(jnp.int32, shape, 0) - OV
        slab_rows = rows - 2 * OV
        depth_low = depth_ref[0]
        depth_high = depth_ref[1]
        act = jnp.where(
            (offsets >= -depth_low) & (offsets < slab_rows + depth_high), 1.0, 0.0
        )
        act_high = jnp.where(
            (offsets + 1 >= -depth_low) & (offsets + 1 < slab_rows + depth_high) & (offsets + 1 < rows - OV),
            1.0,
            0.0,
        )
        lane_end = lax.broadcasted_iota(jnp.int32, shape, 2) % BL != BL - 1
        row_end = (offsets + OV) % BL != BL - 1
        zu_ref[...] = jnp.where(row_end, -fa_ref[...] * act * act_high, 0.0)

        def row_lower(x):
            return jnp.concatenate([jnp.zeros_like(x[:1]), x[:-1]], axis=0)

        def row_upper(x):
            return jnp.concatenate([x[1:], jnp.zeros_like(x[:1])], axis=0)

        def operate(e):
            coupled = (
                fb_ref[...] * row_lower(e)
                + fa_ref[...] * row_upper(e)
                + fl_ref[...] * pltpu.roll(e, 1, 1)
                + fr_ref[...] * pltpu.roll(e, cols - 1, 1)
                + ff_ref[...] * pltpu.roll(e, 1, 2)
                + fk_ref[...] * pltpu.roll(e, lanes - 1, 2)
            )
            return d_ref[...] * e - coupled

        def roll_solve(rhs, m, inv, u, axis, extent):
            forward = rhs
            for _ in range(BL - 1):
                forward = rhs - m * pltpu.roll(forward, 1, axis)
            result = forward * inv
            for _ in range(BL - 1):
                result = (forward - u * pltpu.roll(result, extent - 1, axis)) * inv
            return result

        target = t_ref[...]
        e = jnp.concatenate([left_ref[...], own_ref[...], right_ref[...]], axis=1)
        upper_y = jnp.where(lane_end, -fk_ref[...] * act * act, 0.0)
        update = act * (target - operate(e))
        e = e + weight_now * roll_solve(update, ym_ref[...], yi_ref[...], upper_y, 2, lanes)
        s_ref[...] = act * (target - operate(e))
        for block in range(rows // BL):
            base = block * BL
            forward = s_ref[base]
            f_ref[base] = forward
            for position in range(1, BL):
                r = base + position
                forward = s_ref[r] - zm_ref[r] * forward
                f_ref[r] = forward
            result = forward * zi_ref[base + BL - 1]
            s_ref[base + BL - 1] = result
            for position in range(BL - 2, -1, -1):
                r = base + position
                result = (f_ref[r] - zu_ref[r] * result) * zi_ref[r]
                s_ref[r] = result
        e = e + weight_now * s_ref[...]
        if last:
            o_ref[...] = e
        else:
            update = (act * (target - operate(e)))[:, own_cols]
            own_act = act[:, own_cols]
            col_end = lax.broadcasted_iota(jnp.int32, update.shape, 1) % BL != BL - 1
            upper_x = jnp.where(col_end, -fr_ref[:, own_cols] * own_act * own_act, 0.0)
            o_ref[...] = e[:, own_cols] + weight_next * roll_solve(
                update, xm_ref[...], xi_ref[...], upper_x, 1, BL
            )

    return kernel


def round_call(weight_now, weight_next, last, depths, pieces, target, coeffs, fy, fz, fx):
    tile_cols = pieces[1].shape[1]
    ghost = pieces[0].shape[1]
    own_cols = slice(ghost, ghost + tile_cols)
    shape = target.shape
    out_shape = shape if last else pieces[1].shape
    vmem = pl.BlockSpec(memory_space=pltpu.VMEM)
    return pl.pallas_call(
        make_round_kernel(weight_now, weight_next, last, own_cols),
        out_shape=jax.ShapeDtypeStruct(out_shape, jnp.float32),
        in_specs=[pl.BlockSpec(memory_space=pltpu.SMEM)] + [vmem] * 17,
        out_specs=vmem,
        scratch_shapes=[pltpu.VMEM(shape, jnp.float32)] * 3,
    )(depths, *pieces, target, *coeffs, *fy[:2], *fz[:2], *fx[:2])


def grp_pairs(axis, by):
    devices = lax.axis_size(axis)
    return [(i, i + by) for i in range(devices) if 0 <= i + by < devices]


def with_sides(value, axis, dim):
    from_left = lax.ppermute(value, axis, grp_pairs(axis, 1))
    from_right = lax.ppermute(value, axis, grp_pairs(axis, -1))
    return jnp.concatenate([from_left, value, from_right], axis=dim)


def with_rows(value, axis, dim, width):
    length = value.shape[dim]
    below = lax.ppermute(
        lax.slice_in_dim(value, length - width, length, axis=dim), axis, grp_pairs(axis, 1)
    )
    above = lax.ppermute(lax.slice_in_dim(value, 0, width, axis=dim), axis, grp_pairs(axis, -1))
    return jnp.concatenate([below, value, above], axis=dim)


def with_halo(value, width):
    subs, grps = lax.axis_size("sub"), lax.axis_size("grp")
    top = value[:, -width:]
    bottom = value[:, :width]

    def diagonal(part, dsub, dgrp):
        pairs = [
            (s * grps + g, (s + dsub) * grps + g + dgrp)
            for s in range(subs)
            for g in range(grps)
            if 0 <= s + dsub < subs and 0 <= g + dgrp < grps
        ]
        return lax.ppermute(part, ("sub", "grp"), pairs)

    middle = jnp.concatenate(
        [
            lax.ppermute(top, "sub", grp_pairs("sub", 1)),
            value,
            lax.ppermute(bottom, "sub", grp_pairs("sub", -1)),
        ],
        axis=1,
    )
    left = jnp.concatenate(
        [
            diagonal(top, 1, 1),
            lax.ppermute(value, "grp", grp_pairs("grp", 1)),
            diagonal(bottom, -1, 1),
        ],
        axis=1,
    )
    right = jnp.concatenate(
        [
            diagonal(top, 1, -1),
            lax.ppermute(value, "grp", grp_pairs("grp", -1)),
            diagonal(bottom, -1, -1),
        ],
        axis=1,
    )
    return jnp.concatenate([left, middle, right], axis=2)


def on_device(facies, facies_perm, perm_scale, source, pressure_start, intersection_depth):
    slab_rows, tile_cols, line_cells = source.shape
    margin_rows = slab_rows + 2 * OV
    perm_local = jnp.zeros(source.shape, jnp.float32)
    for facies_kind in range(FACIES):
        perm_local = perm_local + jnp.where(facies == facies_kind, facies_perm[facies_kind], 0.0)
    perm_local = perm_local * perm_scale

    stacked = jnp.stack([perm_local, pressure_start, source])
    stacked = with_rows(stacked, "sub", 1, OV + 1)
    stacked = with_sides(stacked, "grp", 2)
    perm_wide = stacked[0]
    pressure_wide = stacked[1]
    source_wide = stacked[2][1:-1]

    faces_vertical = harmonic(perm_wide[:-1], perm_wide[1:])
    middle_block = perm_wide[1:-1]
    faces_across = harmonic(middle_block[:, :-1], middle_block[:, 1:])
    faces_along = harmonic(middle_block[:, :, :-1], middle_block[:, :, 1:])
    zero_col = jnp.zeros_like(middle_block[:, :1])
    zero_lane = jnp.zeros_like(middle_block[:, :, :1])
    face_below = faces_vertical[:-1]
    face_above = faces_vertical[1:]
    face_left = jnp.concatenate([zero_col, faces_across], axis=1)
    face_right = jnp.concatenate([faces_across, zero_col], axis=1)
    face_front = jnp.concatenate([zero_lane, faces_along], axis=2)
    face_back = jnp.concatenate([faces_along, zero_lane], axis=2)
    diagonal = STORE + face_below + face_above + face_left + face_right + face_front + face_back
    coeffs = (diagonal, face_below, face_above, face_left, face_right, face_front, face_back)
    own = slice(tile_cols, 2 * tile_cols)
    own_coeffs = tuple(member[:, own] for member in coeffs)

    slab_index = lax.axis_index("sub")
    bounds = jnp.concatenate(
        [jnp.zeros((1,), jnp.int32), intersection_depth, jnp.zeros((1,), jnp.int32)]
    )
    depth_low = bounds[slab_index]
    depth_high = bounds[slab_index + 1]
    depths = jnp.stack([depth_low, depth_high])
    offsets = jnp.arange(margin_rows, dtype=jnp.int32) - OV
    inside_slab = (offsets >= -depth_low) & (offsets < slab_rows + depth_high)
    band_rows = (offsets < depth_low) | (offsets >= slab_rows - depth_high)
    active = jnp.where(inside_slab, 1.0, 0.0).reshape(margin_rows, 1, 1)
    weight = jnp.where(inside_slab & band_rows, 0.5, jnp.where(inside_slab, 1.0, 0.0)).reshape(
        margin_rows, 1, 1
    )
    full_active = jnp.broadcast_to(active, diagonal.shape)
    own_active = jnp.broadcast_to(active, own_coeffs[0].shape)
    factors_x = line_factors(own_coeffs, own_active, 1)
    factors_y = line_factors(coeffs, full_active, 2)
    factors_z = line_factors(coeffs, full_active, 0)

    rows_pad = jnp.zeros_like(pressure_wide[:1])
    for outer_turn in range(OUTER):
        center = pressure_wide[1:-1]
        coupled = (
            face_below * pressure_wide[:-2]
            + face_above * pressure_wide[2:]
            + face_left * lower_nb(center, 1)
            + face_right * upper_nb(center, 1)
            + face_front * lower_nb(center, 2)
            + face_back * upper_nb(center, 2)
        )
        residual = source_wide - (diagonal * center - coupled)
        target = residual * active
        estimate_own = relax_weight(0) * solve_lines(factors_x, target[:, own])
        for round_index in range(ROUNDS):
            last = round_index + 1 == ROUNDS
            ghost = tile_cols if (last and outer_turn + 1 < OUTER) else tile_cols // 2
            window = slice(tile_cols - ghost, 2 * tile_cols + ghost)
            pieces = (
                lax.ppermute(estimate_own[:, tile_cols - ghost :], "grp", grp_pairs("grp", 1)),
                estimate_own,
                lax.ppermute(estimate_own[:, :ghost], "grp", grp_pairs("grp", -1)),
            )
            estimate = round_call(
                relax_weight(round_index),
                0.0 if last else relax_weight(round_index + 1),
                last,
                depths,
                pieces,
                target[:, window],
                tuple(member[:, window] for member in coeffs),
                tuple(member[:, window] for member in factors_y[:2]),
                tuple(member[:, window] for member in factors_z[:2]),
                factors_x,
            )
            estimate_own = estimate
        correction = weight * estimate
        if outer_turn + 1 < OUTER:
            span = 2 * OV + 1
            from_below = lax.ppermute(
                correction[margin_rows - span :], "sub", grp_pairs("sub", 1)
            )
            from_above = lax.ppermute(correction[:span], "sub", grp_pairs("sub", -1))
            filler = jnp.zeros(
                (margin_rows + 2 - span,) + correction.shape[1:], jnp.float32
            )
            pressure_wide = (
                pressure_wide
                + jnp.concatenate([rows_pad, correction, rows_pad], axis=0)
                + jnp.concatenate([from_below, filler], axis=0)
                + jnp.concatenate([filler, from_above], axis=0)
            )
        else:
            own_corr = correction[:, ghost : ghost + tile_cols]
            from_below = lax.ppermute(
                own_corr[margin_rows - OV :], "sub", grp_pairs("sub", 1)
            )
            from_above = lax.ppermute(own_corr[:OV], "sub", grp_pairs("sub", -1))
            filler = jnp.zeros((slab_rows - OV, tile_cols, line_cells), jnp.float32)
            combined = (
                own_corr[OV : OV + slab_rows]
                + jnp.concatenate([from_below, filler], axis=0)
                + jnp.concatenate([filler, from_above], axis=0)
            )
            return pressure_wide[OV + 1 : OV + 1 + slab_rows, own] + combined


def solution(mesh):
    return jax.shard_map(
        on_device,
        mesh=mesh,
        in_specs=(
            P("sub", "grp", None),
            P(),
            P("sub", "grp", None),
            P("sub", "grp", None),
            P("sub", "grp", None),
            P(),
        ),
        out_specs=P("sub", "grp", None),
        check_vma=False,
    )
```

```python
import math

import jax
import jax.numpy as jnp
from jax import lax
from jax.sharding import PartitionSpec as P
from jax.experimental import pallas as pl
from jax.experimental.pallas import tpu as pltpu

OV = 4
BL = 8
ROUNDS = 4
OUTER = 2
FACIES = 8


STORE = 0.02


def relax_weight(round_index):
    return 1.0 / (1.4 + 0.6 * math.cos(math.pi * (2 * round_index + 1) / (2 * ROUNDS)))


def harmonic(former, second):
    inside = jnp.where((former > 0) & (second > 0), 1.0, 0.0)
    safe_former = jnp.where(former > 0, former, 1.0)
    safe_second = jnp.where(second > 0, second, 1.0)
    return inside * (2.0 * safe_former * safe_second / (safe_former + safe_second))


def lower_nb(field, axis, fill=0.0):
    extent = field.shape[axis]
    plane = jnp.full_like(lax.slice_in_dim(field, 0, 1, axis=axis), fill)
    return jnp.concatenate([plane, lax.slice_in_dim(field, 0, extent - 1, axis=axis)], axis=axis)


def upper_nb(field, axis, fill=0.0):
    extent = field.shape[axis]
    plane = jnp.full_like(lax.slice_in_dim(field, 0, 1, axis=axis), fill)
    return jnp.concatenate([lax.slice_in_dim(field, 1, extent, axis=axis), plane], axis=axis)


def apply_operator(coeffs, center):
    diagonal, face_below, face_above, face_left, face_right, face_front, face_back = coeffs
    coupled = (
        face_below * lower_nb(center, 0)
        + face_above * upper_nb(center, 0)
        + face_left * lower_nb(center, 1)
        + face_right * upper_nb(center, 1)
        + face_front * lower_nb(center, 2)
        + face_back * upper_nb(center, 2)
    )
    return diagonal * center - coupled


def block_position(shape, axis):
    broadcast_shape = [1] * len(shape)
    broadcast_shape[axis] = shape[axis]
    return (jnp.arange(shape[axis], dtype=jnp.int32) % BL).reshape(broadcast_shape)


def factor_lines(lower_band, middle, upper_band, axis):
    upper_prev = lower_nb(upper_band, axis)
    pivots = middle
    for _ in range(BL - 1):
        pivots = middle - (lower_band / lower_nb(pivots, axis, 1.0)) * upper_prev
    multipliers = lower_band / lower_nb(pivots, axis, 1.0)
    return (multipliers, 1.0 / pivots, upper_band, axis)


def solve_lines(factors, rhs):
    multipliers, inverse, upper_band, axis = factors
    forward = rhs
    for _ in range(BL - 1):
        forward = rhs - multipliers * lower_nb(forward, axis)
    result = forward * inverse
    for _ in range(BL - 1):
        result = (forward - upper_band * upper_nb(result, axis)) * inverse
    return result


def line_factors(coeffs, active, axis):
    diagonal = coeffs[0]
    line_axis = {0: 0, 1: 1, 2: 2}[axis]
    face_low = coeffs[2 * line_axis + 1]
    face_high = coeffs[2 * line_axis + 2]
    position = block_position(diagonal.shape, axis)
    if axis == 0:
        active_low = lower_nb(active, 0)
        active_high = upper_nb(active, 0)
    else:
        active_low = active
        active_high = active
    lower_band = jnp.where(position != 0, -face_low * active * active_low, 0.0)
    upper_band = jnp.where(position != BL - 1, -face_high * active * active_high, 0.0)
    middle = jnp.where(active > 0, diagonal, 1.0)
    return factor_lines(lower_band, middle, upper_band, axis)


def make_round_kernel(weight_now, weight_next, last, own_cols):
    def kernel(
        depth_ref, left_ref, own_ref, right_ref, t_ref, d_ref, fb_ref, fa_ref, fl_ref, fr_ref,
        ff_ref, fk_ref, ym_ref, yi_ref, zm_ref, zi_ref, xm_ref, xi_ref,
        o_ref, s_ref, f_ref, zu_ref,
    ):
        rows, cols, lanes = t_ref.shape
        shape = (rows, cols, lanes)
        offsets = lax.broadcasted_iota(jnp.int32, shape, 0) - OV
        slab_rows = rows - 2 * OV
        depth_low = depth_ref[0]
        depth_high = depth_ref[1]
        act = jnp.where(
            (offsets >= -depth_low) & (offsets < slab_rows + depth_high), 1.0, 0.0
        )
        act_high = jnp.where(
            (offsets + 1 >= -depth_low) & (offsets + 1 < slab_rows + depth_high) & (offsets + 1 < rows - OV),
            1.0,
            0.0,
        )
        lane_end = lax.broadcasted_iota(jnp.int32, shape, 2) % BL != BL - 1
        row_end = (offsets + OV) % BL != BL - 1
        zu_ref[...] = jnp.where(row_end, -fa_ref[...] * act * act_high, 0.0)

        def row_lower(x):
            return jnp.concatenate([jnp.zeros_like(x[:1]), x[:-1]], axis=0)

        def row_upper(x):
            return jnp.concatenate([x[1:], jnp.zeros_like(x[:1])], axis=0)

        def operate(e):
            coupled = (
                fb_ref[...] * row_lower(e)
                + fa_ref[...] * row_upper(e)
                + fl_ref[...] * pltpu.roll(e, 1, 1)
                + fr_ref[...] * pltpu.roll(e, cols - 1, 1)
                + ff_ref[...] * pltpu.roll(e, 1, 2)
                + fk_ref[...] * pltpu.roll(e, lanes - 1, 2)
            )
            return d_ref[...] * e - coupled

        def roll_solve(rhs, m, inv, u, axis, extent):
            forward = rhs
            for _ in range(BL - 1):
                forward = rhs - m * pltpu.roll(forward, 1, axis)
            result = forward * inv
            for _ in range(BL - 1):
                result = (forward - u * pltpu.roll(result, extent - 1, axis)) * inv
            return result

        target = t_ref[...]
        e = jnp.concatenate([left_ref[...], own_ref[...], right_ref[...]], axis=1)
        upper_y = jnp.where(lane_end, -fk_ref[...] * act * act, 0.0)
        update = act * (target - operate(e))
        e = e + weight_now * roll_solve(update, ym_ref[...], yi_ref[...], upper_y, 2, lanes)
        s_ref[...] = act * (target - operate(e))
        for block in range(rows // BL):
            base = block * BL
            forward = s_ref[base]
            f_ref[base] = forward
            for position in range(1, BL):
                r = base + position
                forward = s_ref[r] - zm_ref[r] * forward
                f_ref[r] = forward
            result = forward * zi_ref[base + BL - 1]
            s_ref[base + BL - 1] = result
            for position in range(BL - 2, -1, -1):
                r = base + position
                result = (f_ref[r] - zu_ref[r] * result) * zi_ref[r]
                s_ref[r] = result
        e = e + weight_now * s_ref[...]
        if last:
            o_ref[...] = e
        else:
            update = (act * (target - operate(e)))[:, own_cols]
            own_act = act[:, own_cols]
            col_end = lax.broadcasted_iota(jnp.int32, update.shape, 1) % BL != BL - 1
            upper_x = jnp.where(col_end, -fr_ref[:, own_cols] * own_act * own_act, 0.0)
            o_ref[...] = e[:, own_cols] + weight_next * roll_solve(
                update, xm_ref[...], xi_ref[...], upper_x, 1, BL
            )

    return kernel


def round_call(weight_now, weight_next, last, depths, pieces, target, coeffs, fy, fz, fx):
    tile_cols = pieces[1].shape[1]
    own_cols = slice(tile_cols, 2 * tile_cols)
    shape = target.shape
    out_shape = shape if last else pieces[1].shape
    vmem = pl.BlockSpec(memory_space=pltpu.VMEM)
    return pl.pallas_call(
        make_round_kernel(weight_now, weight_next, last, own_cols),
        out_shape=jax.ShapeDtypeStruct(out_shape, jnp.float32),
        in_specs=[pl.BlockSpec(memory_space=pltpu.SMEM)] + [vmem] * 17,
        out_specs=vmem,
        scratch_shapes=[pltpu.VMEM(shape, jnp.float32)] * 3,
    )(depths, *pieces, target, *coeffs, *fy[:2], *fz[:2], *fx[:2])


def grp_pairs(axis, by):
    devices = lax.axis_size(axis)
    return [(i, i + by) for i in range(devices) if 0 <= i + by < devices]


def with_sides(value, axis, dim):
    from_left = lax.ppermute(value, axis, grp_pairs(axis, 1))
    from_right = lax.ppermute(value, axis, grp_pairs(axis, -1))
    return jnp.concatenate([from_left, value, from_right], axis=dim)


def with_rows(value, axis, dim, width):
    length = value.shape[dim]
    below = lax.ppermute(
        lax.slice_in_dim(value, length - width, length, axis=dim), axis, grp_pairs(axis, 1)
    )
    above = lax.ppermute(lax.slice_in_dim(value, 0, width, axis=dim), axis, grp_pairs(axis, -1))
    return jnp.concatenate([below, value, above], axis=dim)


def with_halo(value, width):
    subs, grps = lax.axis_size("sub"), lax.axis_size("grp")
    top = value[:, -width:]
    bottom = value[:, :width]

    def diagonal(part, dsub, dgrp):
        pairs = [
            (s * grps + g, (s + dsub) * grps + g + dgrp)
            for s in range(subs)
            for g in range(grps)
            if 0 <= s + dsub < subs and 0 <= g + dgrp < grps
        ]
        return lax.ppermute(part, ("sub", "grp"), pairs)

    middle = jnp.concatenate(
        [
            lax.ppermute(top, "sub", grp_pairs("sub", 1)),
            value,
            lax.ppermute(bottom, "sub", grp_pairs("sub", -1)),
        ],
        axis=1,
    )
    left = jnp.concatenate(
        [
            diagonal(top, 1, 1),
            lax.ppermute(value, "grp", grp_pairs("grp", 1)),
            diagonal(bottom, -1, 1),
        ],
        axis=1,
    )
    right = jnp.concatenate(
        [
            diagonal(top, 1, -1),
            lax.ppermute(value, "grp", grp_pairs("grp", -1)),
            diagonal(bottom, -1, -1),
        ],
        axis=1,
    )
    return jnp.concatenate([left, middle, right], axis=2)


def on_device(facies, facies_perm, perm_scale, source, pressure_start, intersection_depth):
    slab_rows, tile_cols, line_cells = source.shape
    margin_rows = slab_rows + 2 * OV
    kinds = jnp.arange(FACIES, dtype=jnp.int32).reshape(FACIES, 1, 1, 1)
    table = facies_perm.reshape(FACIES, 1, 1, 1)
    perm_local = jnp.sum(jnp.where(facies[None] == kinds, table, 0.0), axis=0) * perm_scale

    stacked = jnp.stack([perm_local, pressure_start, source])
    stacked = with_rows(stacked, "sub", 1, OV + 1)
    stacked = with_sides(stacked, "grp", 2)
    perm_wide = stacked[0]
    pressure_wide = stacked[1]
    source_wide = stacked[2][1:-1]

    faces_vertical = harmonic(perm_wide[:-1], perm_wide[1:])
    middle_block = perm_wide[1:-1]
    faces_across = harmonic(middle_block[:, :-1], middle_block[:, 1:])
    faces_along = harmonic(middle_block[:, :, :-1], middle_block[:, :, 1:])
    zero_col = jnp.zeros_like(middle_block[:, :1])
    zero_lane = jnp.zeros_like(middle_block[:, :, :1])
    face_below = faces_vertical[:-1]
    face_above = faces_vertical[1:]
    face_left = jnp.concatenate([zero_col, faces_across], axis=1)
    face_right = jnp.concatenate([faces_across, zero_col], axis=1)
    face_front = jnp.concatenate([zero_lane, faces_along], axis=2)
    face_back = jnp.concatenate([faces_along, zero_lane], axis=2)
    diagonal = STORE + face_below + face_above + face_left + face_right + face_front + face_back
    coeffs = (diagonal, face_below, face_above, face_left, face_right, face_front, face_back)
    own = slice(tile_cols, 2 * tile_cols)
    own_coeffs = tuple(member[:, own] for member in coeffs)

    slab_index = lax.axis_index("sub")
    bounds = jnp.concatenate(
        [jnp.zeros((1,), jnp.int32), intersection_depth, jnp.zeros((1,), jnp.int32)]
    )
    depth_low = bounds[slab_index]
    depth_high = bounds[slab_index + 1]
    depths = jnp.stack([depth_low, depth_high])
    offsets = jnp.arange(margin_rows, dtype=jnp.int32) - OV
    inside_slab = (offsets >= -depth_low) & (offsets < slab_rows + depth_high)
    band_rows = (offsets < depth_low) | (offsets >= slab_rows - depth_high)
    active = jnp.where(inside_slab, 1.0, 0.0).reshape(margin_rows, 1, 1)
    weight = jnp.where(inside_slab & band_rows, 0.5, jnp.where(inside_slab, 1.0, 0.0)).reshape(
        margin_rows, 1, 1
    )
    full_active = jnp.broadcast_to(active, diagonal.shape)
    own_active = jnp.broadcast_to(active, own_coeffs[0].shape)
    factors_x = line_factors(own_coeffs, own_active, 1)
    factors_y = line_factors(coeffs, full_active, 2)
    factors_z = line_factors(coeffs, full_active, 0)

    rows_pad = jnp.zeros_like(pressure_wide[:1])
    for outer_turn in range(OUTER):
        center = pressure_wide[1:-1]
        coupled = (
            face_below * pressure_wide[:-2]
            + face_above * pressure_wide[2:]
            + face_left * lower_nb(center, 1)
            + face_right * upper_nb(center, 1)
            + face_front * lower_nb(center, 2)
            + face_back * upper_nb(center, 2)
        )
        residual = source_wide - (diagonal * center - coupled)
        target = residual * active
        estimate_own = relax_weight(0) * solve_lines(factors_x, target[:, own])
        for round_index in range(ROUNDS):
            pieces = (
                lax.ppermute(estimate_own, "grp", grp_pairs("grp", 1)),
                estimate_own,
                lax.ppermute(estimate_own, "grp", grp_pairs("grp", -1)),
            )
            last = round_index + 1 == ROUNDS
            estimate = round_call(
                relax_weight(round_index),
                0.0 if last else relax_weight(round_index + 1),
                last,
                depths,
                pieces,
                target,
                coeffs,
                factors_y,
                factors_z,
                factors_x,
            )
            estimate_own = estimate
        correction = weight * estimate
        if outer_turn + 1 < OUTER:
            span = 2 * OV + 1
            from_below = lax.ppermute(
                correction[margin_rows - span :], "sub", grp_pairs("sub", 1)
            )
            from_above = lax.ppermute(correction[:span], "sub", grp_pairs("sub", -1))
            filler = jnp.zeros(
                (margin_rows + 2 - span,) + correction.shape[1:], jnp.float32
            )
            pressure_wide = (
                pressure_wide
                + jnp.concatenate([rows_pad, correction, rows_pad], axis=0)
                + jnp.concatenate([from_below, filler], axis=0)
                + jnp.concatenate([filler, from_above], axis=0)
            )
        else:
            own_corr = correction[:, own]
            from_below = lax.ppermute(
                own_corr[margin_rows - OV :], "sub", grp_pairs("sub", 1)
            )
            from_above = lax.ppermute(own_corr[:OV], "sub", grp_pairs("sub", -1))
            filler = jnp.zeros((slab_rows - OV, tile_cols, line_cells), jnp.float32)
            combined = (
                own_corr[OV : OV + slab_rows]
                + jnp.concatenate([from_below, filler], axis=0)
                + jnp.concatenate([filler, from_above], axis=0)
            )
            return pressure_wide[OV + 1 : OV + 1 + slab_rows, own] + combined


def solution(mesh):
    return jax.shard_map(
        on_device,
        mesh=mesh,
        in_specs=(
            P("sub", "grp", None),
            P(),
            P("sub", "grp", None),
            P("sub", "grp", None),
            P("sub", "grp", None),
            P(),
        ),
        out_specs=P("sub", "grp", None),
        check_vma=False,
    )
```

```python
import math

import jax
import jax.numpy as jnp
from jax import lax
from jax.sharding import PartitionSpec as P
from jax.experimental import pallas as pl
from jax.experimental.pallas import tpu as pltpu

OV = 4
BL = 8
ROUNDS = 4
OUTER = 2
FACIES = 8


STORE = 0.02


def relax_weight(round_index):
    return 1.0 / (1.4 + 0.6 * math.cos(math.pi * (2 * round_index + 1) / (2 * ROUNDS)))


def harmonic(former, second):
    inside = jnp.where((former > 0) & (second > 0), 1.0, 0.0)
    safe_former = jnp.where(former > 0, former, 1.0)
    safe_second = jnp.where(second > 0, second, 1.0)
    return inside * (2.0 * safe_former * safe_second / (safe_former + safe_second))


def lower_nb(field, axis, fill=0.0):
    extent = field.shape[axis]
    plane = jnp.full_like(lax.slice_in_dim(field, 0, 1, axis=axis), fill)
    return jnp.concatenate([plane, lax.slice_in_dim(field, 0, extent - 1, axis=axis)], axis=axis)


def upper_nb(field, axis, fill=0.0):
    extent = field.shape[axis]
    plane = jnp.full_like(lax.slice_in_dim(field, 0, 1, axis=axis), fill)
    return jnp.concatenate([lax.slice_in_dim(field, 1, extent, axis=axis), plane], axis=axis)


def apply_operator(coeffs, center):
    diagonal, face_below, face_above, face_left, face_right, face_front, face_back = coeffs
    coupled = (
        face_below * lower_nb(center, 0)
        + face_above * upper_nb(center, 0)
        + face_left * lower_nb(center, 1)
        + face_right * upper_nb(center, 1)
        + face_front * lower_nb(center, 2)
        + face_back * upper_nb(center, 2)
    )
    return diagonal * center - coupled


def block_position(shape, axis):
    broadcast_shape = [1] * len(shape)
    broadcast_shape[axis] = shape[axis]
    return (jnp.arange(shape[axis], dtype=jnp.int32) % BL).reshape(broadcast_shape)


def factor_lines(lower_band, middle, upper_band, axis):
    upper_prev = lower_nb(upper_band, axis)
    pivots = middle
    for _ in range(BL - 1):
        pivots = middle - (lower_band / lower_nb(pivots, axis, 1.0)) * upper_prev
    multipliers = lower_band / lower_nb(pivots, axis, 1.0)
    return (multipliers, 1.0 / pivots, upper_band, axis)


def solve_lines(factors, rhs):
    multipliers, inverse, upper_band, axis = factors
    forward = rhs
    for _ in range(BL - 1):
        forward = rhs - multipliers * lower_nb(forward, axis)
    result = forward * inverse
    for _ in range(BL - 1):
        result = (forward - upper_band * upper_nb(result, axis)) * inverse
    return result


def line_factors(coeffs, active, axis):
    diagonal = coeffs[0]
    line_axis = {0: 0, 1: 1, 2: 2}[axis]
    face_low = coeffs[2 * line_axis + 1]
    face_high = coeffs[2 * line_axis + 2]
    position = block_position(diagonal.shape, axis)
    if axis == 0:
        active_low = lower_nb(active, 0)
        active_high = upper_nb(active, 0)
    else:
        active_low = active
        active_high = active
    lower_band = jnp.where(position != 0, -face_low * active * active_low, 0.0)
    upper_band = jnp.where(position != BL - 1, -face_high * active * active_high, 0.0)
    middle = jnp.where(active > 0, diagonal, 1.0)
    return factor_lines(lower_band, middle, upper_band, axis)


def make_round_kernel(weight_now, weight_next, last, own_cols):
    def kernel(
        depth_ref, left_ref, own_ref, right_ref, t_ref, d_ref, fb_ref, fa_ref, fl_ref, fr_ref,
        ff_ref, fk_ref, ym_ref, yi_ref, zm_ref, zi_ref, xm_ref, xi_ref,
        o_ref, s_ref, f_ref, zu_ref,
    ):
        rows, cols, lanes = t_ref.shape
        shape = (rows, cols, lanes)
        offsets = lax.broadcasted_iota(jnp.int32, shape, 0) - OV
        slab_rows = rows - 2 * OV
        depth_low = depth_ref[0]
        depth_high = depth_ref[1]
        act = jnp.where(
            (offsets >= -depth_low) & (offsets < slab_rows + depth_high), 1.0, 0.0
        )
        act_high = jnp.where(
            (offsets + 1 >= -depth_low) & (offsets + 1 < slab_rows + depth_high) & (offsets + 1 < rows - OV),
            1.0,
            0.0,
        )
        lane_end = lax.broadcasted_iota(jnp.int32, shape, 2) % BL != BL - 1
        row_end = (offsets + OV) % BL != BL - 1
        zu_ref[...] = jnp.where(row_end, -fa_ref[...] * act * act_high, 0.0)

        def row_lower(x):
            return jnp.concatenate([jnp.zeros_like(x[:1]), x[:-1]], axis=0)

        def row_upper(x):
            return jnp.concatenate([x[1:], jnp.zeros_like(x[:1])], axis=0)

        def operate(e):
            coupled = (
                fb_ref[...] * row_lower(e)
                + fa_ref[...] * row_upper(e)
                + fl_ref[...] * pltpu.roll(e, 1, 1)
                + fr_ref[...] * pltpu.roll(e, cols - 1, 1)
                + ff_ref[...] * pltpu.roll(e, 1, 2)
                + fk_ref[...] * pltpu.roll(e, lanes - 1, 2)
            )
            return d_ref[...] * e - coupled

        def roll_solve(rhs, m, inv, u, axis, extent):
            forward = rhs
            for _ in range(BL - 1):
                forward = rhs - m * pltpu.roll(forward, 1, axis)
            result = forward * inv
            for _ in range(BL - 1):
                result = (forward - u * pltpu.roll(result, extent - 1, axis)) * inv
            return result

        target = t_ref[...]
        e = jnp.concatenate([left_ref[...], own_ref[...], right_ref[...]], axis=1)
        upper_y = jnp.where(lane_end, -fk_ref[...] * act * act, 0.0)
        update = act * (target - operate(e))
        e = e + weight_now * roll_solve(update, ym_ref[...], yi_ref[...], upper_y, 2, lanes)
        s_ref[...] = act * (target - operate(e))
        for block in range(rows // BL):
            base = block * BL
            forward = s_ref[base]
            f_ref[base] = forward
            for position in range(1, BL):
                r = base + position
                forward = s_ref[r] - zm_ref[r] * forward
                f_ref[r] = forward
            result = forward * zi_ref[base + BL - 1]
            s_ref[base + BL - 1] = result
            for position in range(BL - 2, -1, -1):
                r = base + position
                result = (f_ref[r] - zu_ref[r] * result) * zi_ref[r]
                s_ref[r] = result
        e = e + weight_now * s_ref[...]
        if last:
            inside = (offsets >= -depth_low) & (offsets < slab_rows + depth_high)
            band = (offsets < depth_low) | (offsets >= slab_rows - depth_high)
            o_ref[...] = jnp.where(inside & band, 0.5, jnp.where(inside, 1.0, 0.0)) * e
        else:
            update = (act * (target - operate(e)))[:, own_cols]
            own_act = act[:, own_cols]
            col_end = lax.broadcasted_iota(jnp.int32, update.shape, 1) % BL != BL - 1
            upper_x = jnp.where(col_end, -fr_ref[:, own_cols] * own_act * own_act, 0.0)
            o_ref[...] = e[:, own_cols] + weight_next * roll_solve(
                update, xm_ref[...], xi_ref[...], upper_x, 1, BL
            )

    return kernel


def round_call(weight_now, weight_next, last, depths, pieces, target, coeffs, fy, fz, fx):
    tile_cols = pieces[1].shape[1]
    own_cols = slice(tile_cols, 2 * tile_cols)
    shape = target.shape
    out_shape = shape if last else pieces[1].shape
    vmem = pl.BlockSpec(memory_space=pltpu.VMEM)
    return pl.pallas_call(
        make_round_kernel(weight_now, weight_next, last, own_cols),
        out_shape=jax.ShapeDtypeStruct(out_shape, jnp.float32),
        in_specs=[pl.BlockSpec(memory_space=pltpu.SMEM)] + [vmem] * 17,
        out_specs=vmem,
        scratch_shapes=[pltpu.VMEM(shape, jnp.float32)] * 3,
    )(depths, *pieces, target, *coeffs, *fy[:2], *fz[:2], *fx[:2])


def grp_pairs(axis, by):
    devices = lax.axis_size(axis)
    return [(i, i + by) for i in range(devices) if 0 <= i + by < devices]


def with_sides(value, axis, dim):
    from_left = lax.ppermute(value, axis, grp_pairs(axis, 1))
    from_right = lax.ppermute(value, axis, grp_pairs(axis, -1))
    return jnp.concatenate([from_left, value, from_right], axis=dim)


def with_rows(value, axis, dim, width):
    length = value.shape[dim]
    below = lax.ppermute(
        lax.slice_in_dim(value, length - width, length, axis=dim), axis, grp_pairs(axis, 1)
    )
    above = lax.ppermute(lax.slice_in_dim(value, 0, width, axis=dim), axis, grp_pairs(axis, -1))
    return jnp.concatenate([below, value, above], axis=dim)


def with_halo(value, width):
    subs, grps = lax.axis_size("sub"), lax.axis_size("grp")
    top = value[:, -width:]
    bottom = value[:, :width]

    def diagonal(part, dsub, dgrp):
        pairs = [
            (s * grps + g, (s + dsub) * grps + g + dgrp)
            for s in range(subs)
            for g in range(grps)
            if 0 <= s + dsub < subs and 0 <= g + dgrp < grps
        ]
        return lax.ppermute(part, ("sub", "grp"), pairs)

    middle = jnp.concatenate(
        [
            lax.ppermute(top, "sub", grp_pairs("sub", 1)),
            value,
            lax.ppermute(bottom, "sub", grp_pairs("sub", -1)),
        ],
        axis=1,
    )
    left = jnp.concatenate(
        [
            diagonal(top, 1, 1),
            lax.ppermute(value, "grp", grp_pairs("grp", 1)),
            diagonal(bottom, -1, 1),
        ],
        axis=1,
    )
    right = jnp.concatenate(
        [
            diagonal(top, 1, -1),
            lax.ppermute(value, "grp", grp_pairs("grp", -1)),
            diagonal(bottom, -1, -1),
        ],
        axis=1,
    )
    return jnp.concatenate([left, middle, right], axis=2)


def on_device(facies, facies_perm, perm_scale, source, pressure_start, intersection_depth):
    slab_rows, tile_cols, line_cells = source.shape
    margin_rows = slab_rows + 2 * OV
    kinds = jnp.arange(FACIES, dtype=jnp.int32).reshape(FACIES, 1, 1, 1)
    table = facies_perm.reshape(FACIES, 1, 1, 1)
    perm_local = jnp.sum(jnp.where(facies[None] == kinds, table, 0.0), axis=0) * perm_scale

    stacked = jnp.stack([perm_local, pressure_start, source])
    stacked = with_rows(stacked, "sub", 1, OV + 1)
    stacked = with_sides(stacked, "grp", 2)
    perm_wide = stacked[0]
    pressure_wide = stacked[1]
    source_wide = stacked[2][1:-1]

    faces_vertical = harmonic(perm_wide[:-1], perm_wide[1:])
    middle_block = perm_wide[1:-1]
    faces_across = harmonic(middle_block[:, :-1], middle_block[:, 1:])
    faces_along = harmonic(middle_block[:, :, :-1], middle_block[:, :, 1:])
    zero_col = jnp.zeros_like(middle_block[:, :1])
    zero_lane = jnp.zeros_like(middle_block[:, :, :1])
    face_below = faces_vertical[:-1]
    face_above = faces_vertical[1:]
    face_left = jnp.concatenate([zero_col, faces_across], axis=1)
    face_right = jnp.concatenate([faces_across, zero_col], axis=1)
    face_front = jnp.concatenate([zero_lane, faces_along], axis=2)
    face_back = jnp.concatenate([faces_along, zero_lane], axis=2)
    diagonal = STORE + face_below + face_above + face_left + face_right + face_front + face_back
    coeffs = (diagonal, face_below, face_above, face_left, face_right, face_front, face_back)
    own = slice(tile_cols, 2 * tile_cols)
    own_coeffs = tuple(member[:, own] for member in coeffs)

    slab_index = lax.axis_index("sub")
    bounds = jnp.concatenate(
        [jnp.zeros((1,), jnp.int32), intersection_depth, jnp.zeros((1,), jnp.int32)]
    )
    depth_low = bounds[slab_index]
    depth_high = bounds[slab_index + 1]
    depths = jnp.stack([depth_low, depth_high])
    offsets = jnp.arange(margin_rows, dtype=jnp.int32) - OV
    inside_slab = (offsets >= -depth_low) & (offsets < slab_rows + depth_high)
    band_rows = (offsets < depth_low) | (offsets >= slab_rows - depth_high)
    active = jnp.where(inside_slab, 1.0, 0.0).reshape(margin_rows, 1, 1)
    weight = jnp.where(inside_slab & band_rows, 0.5, jnp.where(inside_slab, 1.0, 0.0)).reshape(
        margin_rows, 1, 1
    )
    full_active = jnp.broadcast_to(active, diagonal.shape)
    own_active = jnp.broadcast_to(active, own_coeffs[0].shape)
    factors_x = line_factors(own_coeffs, own_active, 1)
    factors_y = line_factors(coeffs, full_active, 2)
    factors_z = line_factors(coeffs, full_active, 0)

    rows_pad = jnp.zeros_like(pressure_wide[:1])
    for outer_turn in range(OUTER):
        center = pressure_wide[1:-1]
        coupled = (
            face_below * pressure_wide[:-2]
            + face_above * pressure_wide[2:]
            + face_left * lower_nb(center, 1)
            + face_right * upper_nb(center, 1)
            + face_front * lower_nb(center, 2)
            + face_back * upper_nb(center, 2)
        )
        residual = source_wide - (diagonal * center - coupled)
        target = residual * active
        estimate_own = relax_weight(0) * solve_lines(factors_x, target[:, own])
        for round_index in range(ROUNDS):
            pieces = (
                lax.ppermute(estimate_own, "grp", grp_pairs("grp", 1)),
                estimate_own,
                lax.ppermute(estimate_own, "grp", grp_pairs("grp", -1)),
            )
            last = round_index + 1 == ROUNDS
            estimate = round_call(
                relax_weight(round_index),
                0.0 if last else relax_weight(round_index + 1),
                last,
                depths,
                pieces,
                target,
                coeffs,
                factors_y,
                factors_z,
                factors_x,
            )
            estimate_own = estimate
        correction = estimate
        if outer_turn + 1 < OUTER:
            span = 2 * OV + 1
            from_below = lax.ppermute(
                correction[margin_rows - span :], "sub", grp_pairs("sub", 1)
            )
            from_above = lax.ppermute(correction[:span], "sub", grp_pairs("sub", -1))
            filler = jnp.zeros(
                (margin_rows + 2 - span,) + correction.shape[1:], jnp.float32
            )
            pressure_wide = (
                pressure_wide
                + jnp.concatenate([rows_pad, correction, rows_pad], axis=0)
                + jnp.concatenate([from_below, filler], axis=0)
                + jnp.concatenate([filler, from_above], axis=0)
            )
        else:
            own_corr = correction[:, own]
            from_below = lax.ppermute(
                own_corr[margin_rows - OV :], "sub", grp_pairs("sub", 1)
            )
            from_above = lax.ppermute(own_corr[:OV], "sub", grp_pairs("sub", -1))
            filler = jnp.zeros((slab_rows - OV, tile_cols, line_cells), jnp.float32)
            combined = (
                own_corr[OV : OV + slab_rows]
                + jnp.concatenate([from_below, filler], axis=0)
                + jnp.concatenate([filler, from_above], axis=0)
            )
            return pressure_wide[OV + 1 : OV + 1 + slab_rows, own] + combined


def solution(mesh):
    return jax.shard_map(
        on_device,
        mesh=mesh,
        in_specs=(
            P("sub", "grp", None),
            P(),
            P("sub", "grp", None),
            P("sub", "grp", None),
            P("sub", "grp", None),
            P(),
        ),
        out_specs=P("sub", "grp", None),
        check_vma=False,
    )
```
